256 devices in a mesh: dp: 32 (over x, y, core), expert: 8 (over z).
Axes of the slice: x: 4, y: 4, z: 8, core: 2. Of those that a mesh axis runs over, the one named last changes fastest.
Arguments:
- tokens: bfloat16 [32768, 2048], P(('dp', 'expert')), may hold values from -6 to 6
- expert_ids: int32 [32768, 3], P(('dp', 'expert')), may hold values from 0 to 7, as said below
- slot_index: int32 [32768, 3], P(('dp', 'expert')), may hold values from -1 to 47, as said below
- w_router: float32 [2048, 8], replicated, may hold values from -0.125 to 0.125
- w_gate: bfloat16 [8, 2048, 768], P('expert'), may hold values from -0.125 to 0.125
- w_up: bfloat16 [8, 2048, 768], P('expert'), may hold values from -0.125 to 0.125
- w_down: bfloat16 [8, 2048, 768], P('expert'), may hold values from -0.21875 to 0.21875
- grad_out: bfloat16 [32768, 2048], P(('dp', 'expert')), may hold values from -0.59765625 to 0.59765625
Outputs:
- layer_output: bfloat16 [32768, 2048], P(('dp', 'expert'))
- grad_tokens: bfloat16 [32768, 2048], P(('dp', 'expert'))
- grad_router: float32 [2048, 8], replicated
- grad_gate: float32 [8, 2048, 768], P('expert', 'dp')
- grad_up: float32 [8, 2048, 768], P('expert', 'dp')
- grad_down: float32 [8, 2048, 768], P('expert', 'dp')
The draws below stay inside these ranges and needn't reach their ends.
Inputs may be any that keep to these rules, and one draw needn't show every extreme that they name: `expert_ids`: each token names 3 different experts. `slot_index`: the live choices of one device's 128 tokens to one expert take the slots 0, 1, 2, ... in the order of tokens and then choices, and choices past 48 of them get -1; in every draw some expert gets all 48 slots from every device.
All inputs are finite; a program needn't handle non-finite values.
Results may differ from the reference program's by a relative error of at most 0.025.
Values may be sent and summed in bfloat16 or wider, within the bound.
No kernel may reach another device: no remote copies, remote signals or barrier semaphores. Data moves between devices by JAX's collectives and lax.ppermute only.
A program may use at most 128 MiB of HBM per device.

```python
import jax
import jax.numpy as jnp
from jax import lax

D = 2048
FF = 768
TOP = 3
TOK_DEV = 128
EXPERTS = 8
TOKENS = 32768
CAP = 48
N_DP = 32
N_EXPERT = 8


def routing(key):
    pop_key = jax.random.fold_in(key, 71)
    noise_key = jax.random.fold_in(key, 72)
    popular = jax.random.randint(pop_key, (EXPERTS,), 0, 1600, dtype=jnp.int32)
    noise_draw = jax.random.randint(noise_key, (TOKENS, EXPERTS), 0, 4000, dtype=jnp.int32)
    ranked = (noise_draw + popular[None, :]) * EXPERTS + jnp.arange(EXPERTS, dtype=jnp.int32)[None, :]
    _, chosen = lax.top_k(ranked, TOP)
    chosen = chosen.astype(jnp.int32)
    onehot = (chosen[:, :, None] == jnp.arange(EXPERTS, dtype=jnp.int32)[None, None, :]).astype(jnp.int32)
    block_view = onehot.reshape(TOKENS // TOK_DEV, TOK_DEV * TOP, EXPERTS)
    rank_table = jnp.cumsum(block_view, axis=1) - 1
    position = jnp.sum(rank_table * block_view, axis=2).reshape(TOKENS, TOP)
    slot_index = jnp.where(position < CAP, position, -1).astype(jnp.int32)
    return (chosen, slot_index)


def draw_expert_ids(key, part):
    return routing(key)[0]


def draw_slot_index(key, part):
    return routing(key)[1]


def block_scale(key, extent, cuts, low, high):
    level, own = 1.0, jax.random.fold_in(key, 6)
    for dim, blocks in cuts:
        steps = jnp.exp(jax.random.uniform(jax.random.fold_in(own, dim), (blocks,), jnp.float32, low / len(cuts), high / len(cuts)))
        level = level * jnp.repeat(steps, extent[dim] // blocks).reshape([-1 if axis == dim else 1 for axis in range(len(extent))])
    return level


def noise(own_key, shape, spread, most, pieces=(), kind=jnp.bfloat16):
    level = block_scale(own_key, shape, pieces, -0.22, 0.18) if pieces else 1.0
    entries = jax.random.normal(own_key, shape, jnp.float32) * spread * level
    return jnp.minimum(jnp.maximum(entries, -most), most).astype(kind)


def setup_inputs(seed: int = 0) -> dict:
    streams_of = jax.random.split(jax.random.key(seed), 9)
    tokens = noise(streams_of[0], (TOKENS, D), 1.0, 6.0, ((0, 256),))
    expert_ids = draw_expert_ids(jax.random.fold_in(streams_of[8], 71), 0)
    slot_index = draw_slot_index(jax.random.fold_in(streams_of[8], 71), 0)
    w_router = noise(streams_of[3], (D, EXPERTS), D ** -0.5, 0.125, (), jnp.float32)
    w_gate = noise(streams_of[4], (EXPERTS, D, FF), D ** -0.5, 0.125, ((0, 8),))
    w_up = noise(streams_of[5], (EXPERTS, D, FF), D ** -0.5, 0.125, ((0, 8),))
    w_down = noise(streams_of[6], (EXPERTS, D, FF), FF ** -0.5, 0.21875, ((0, 8),))
    grad_out = noise(streams_of[7], (TOKENS, D), 0.1, 0.59765625, ((0, 256),))
    return {"tokens": tokens, "expert_ids": expert_ids, "slot_index": slot_index, "w_router": w_router, "w_gate": w_gate, "w_up": w_up, "w_down": w_down, "grad_out": grad_out}


def silu_parts(hidden):
    sigmoid_val = jax.nn.sigmoid(hidden)
    return hidden * sigmoid_val, sigmoid_val * (1.0 + hidden * (1.0 - sigmoid_val))


def reference(tokens, expert_ids, slot_index, w_router, w_gate, w_up, w_down, grad_out):
    highest = lax.Precision.HIGHEST
    device_count = N_DP * N_EXPERT
    per_expert = device_count * CAP
    group_rows = N_EXPERT * CAP
    tokens_wide = tokens.astype(jnp.float32)
    scores = jax.nn.sigmoid(jnp.dot(tokens_wide, w_router, precision=highest))
    picked = jnp.take_along_axis(scores, expert_ids, axis=1)
    pick_sum = jnp.sum(picked, axis=1, keepdims=True)
    gate_value = picked / pick_sum
    is_live = slot_index >= 0
    live_gate = jnp.where(is_live, gate_value, 0.0)
    device_of = jnp.arange(TOKENS, dtype=jnp.int32) // TOK_DEV
    position = (expert_ids * device_count + device_of[:, None]) * CAP + slot_index
    position = jnp.where(is_live, position, EXPERTS * per_expert).astype(jnp.int32)
    owner_table = jnp.full((EXPERTS * per_expert + 1,), TOKENS * TOP, jnp.int32)
    owner_table = owner_table.at[position.reshape(-1)].set(jnp.arange(TOKENS * TOP, dtype=jnp.int32))
    zero_row = jnp.zeros((1, D), jnp.bfloat16)
    token_pad = jnp.concatenate([tokens, zero_row], axis=0)
    grad_pad = jnp.concatenate([grad_out, zero_row], axis=0)
    gate_pad = jnp.concatenate([live_gate.reshape(-1), jnp.zeros((1,), jnp.float32)])

    def one_expert(expert_idx):
        owned = lax.dynamic_slice_in_dim(owner_table, (expert_idx * per_expert).astype(jnp.int32), per_expert)
        row_block = token_pad[owned // TOP]
        gate_mat = w_gate[expert_idx]
        up_mat = w_up[expert_idx]
        down_mat = w_down[expert_idx]
        hidden_gate = jnp.dot(row_block, gate_mat, preferred_element_type=jnp.float32)
        hidden_up = jnp.dot(row_block, up_mat, preferred_element_type=jnp.float32)
        silu_value, silu_slope = silu_parts(hidden_gate)
        activated = (silu_value * hidden_up).astype(jnp.bfloat16)
        expert_out = jnp.dot(activated, down_mat.T, preferred_element_type=jnp.float32).astype(jnp.bfloat16)
        grad_rows = (gate_pad[owned][:, None] * grad_pad[owned // TOP].astype(jnp.float32)).astype(jnp.bfloat16)
        grad_act = jnp.dot(grad_rows, down_mat, preferred_element_type=jnp.float32)
        gate_delta = (grad_act * hidden_up * silu_slope).astype(jnp.bfloat16)
        up_delta = (grad_act * silu_value).astype(jnp.bfloat16)
        row_grad = (jnp.dot(gate_delta, gate_mat.T, preferred_element_type=jnp.float32)
                    + jnp.dot(up_delta, up_mat.T, preferred_element_type=jnp.float32)).astype(jnp.bfloat16)

        def group_sum(carry, group_idx):
            begin = (group_idx * group_rows).astype(jnp.int32)
            rows_g = lax.dynamic_slice_in_dim(row_block, begin, group_rows)
            gate_g = lax.dynamic_slice_in_dim(gate_delta, begin, group_rows)
            up_g = lax.dynamic_slice_in_dim(up_delta, begin, group_rows)
            grad_g = lax.dynamic_slice_in_dim(grad_rows, begin, group_rows)
            act_g = lax.dynamic_slice_in_dim(activated, begin, group_rows)
            parts = (jnp.dot(rows_g.T, gate_g, preferred_element_type=jnp.float32),
                     jnp.dot(rows_g.T, up_g, preferred_element_type=jnp.float32),
                     jnp.dot(grad_g.T, act_g, preferred_element_type=jnp.float32))
            rounded = tuple(lax.optimization_barrier(piece.astype(jnp.bfloat16)).astype(jnp.float32) for piece in parts)
            return tuple(acc + piece for acc, piece in zip(carry, rounded)), None

        start_sums = tuple(jnp.zeros((D, FF), jnp.float32) for _ in range(3))
        sums, _ = lax.scan(group_sum, start_sums, jnp.arange(N_DP, dtype=jnp.int32))
        return expert_out, row_grad, sums[0], sums[1], sums[2]

    expert_out, row_grad, grad_gate, grad_up, grad_down = lax.map(one_expert, jnp.arange(EXPERTS, dtype=jnp.int32))
    out_pad = jnp.concatenate([expert_out.reshape(-1, D), zero_row], axis=0)
    back_pad = jnp.concatenate([row_grad.reshape(-1, D), zero_row], axis=0)
    dy_wide = grad_out.astype(jnp.float32)
    mixed = jnp.zeros((TOKENS, D), jnp.float32)
    row_sum = jnp.zeros((TOKENS, D), jnp.float32)
    gate_grads = []
    for which in range(TOP):
        got_row = out_pad[position[:, which]].astype(jnp.float32)
        mixed = mixed + live_gate[:, which:which + 1] * got_row
        gate_grads.append(jnp.sum(dy_wide * got_row, axis=1))
        row_sum = row_sum + back_pad[position[:, which]].astype(jnp.float32)
    layer_output = mixed.astype(jnp.bfloat16)
    gate_grad = jnp.stack(gate_grads, axis=1)
    cross_term = jnp.sum(gate_grad * gate_value, axis=1, keepdims=True)
    pick_delta = (gate_grad - cross_term) / pick_sum * picked * (1.0 - picked)
    picker = (expert_ids[:, :, None] == jnp.arange(EXPERTS, dtype=jnp.int32)[None, None, :]).astype(jnp.float32)
    logit_grad = jnp.sum(picker * pick_delta[:, :, None], axis=1)
    grad_router = jnp.dot(tokens_wide.T, logit_grad, precision=highest)
    grad_tokens = (row_sum + jnp.dot(logit_grad, w_router.T, precision=highest)).astype(jnp.bfloat16)
    return layer_output, grad_tokens, grad_router, grad_gate, grad_up, grad_down
```

```python
import jax
import jax.numpy as jnp
from jax import lax
from jax.sharding import PartitionSpec as P


def silu_parts(hidden):
    sigmoid_val = jax.nn.sigmoid(hidden)
    return (hidden * sigmoid_val, sigmoid_val * (1.0 + hidden * (1.0 - sigmoid_val)))


def butterfly_sum(value, axis):
    size = lax.axis_size(axis)
    step = 1
    while step < size:
        pairs = [(i, i ^ step) for i in range(size)]
        value = value + lax.ppermute(value, axis, pairs)
        step *= 2
    return value


def on_device(tokens, expert_ids, slot_index, w_router, w_gate, w_up, w_down, grad_out):
    tok_count, width = tokens.shape
    choice_count = expert_ids.shape[1]
    expert_count = w_router.shape[1]
    local_count = w_gate.shape[0]
    hidden_width = w_gate.shape[2]
    sender_count = lax.axis_size("expert")
    own_rows = width // lax.axis_size("dp")
    slot_count = tok_count * choice_count // expert_count
    highest = lax.Precision.HIGHEST
    tokens_wide = tokens.astype(jnp.float32)
    scores = jax.nn.sigmoid(jnp.dot(tokens_wide, w_router, precision=highest))
    picker = (
        expert_ids[:, :, None] == jnp.arange(expert_count, dtype=jnp.int32)[None, None, :]
    ).astype(jnp.float32)
    picked = jnp.sum(picker * scores[:, None, :], axis=2)
    pick_sum = jnp.sum(picked, axis=1, keepdims=True)
    gate_value = picked / pick_sum
    is_live = slot_index >= 0
    live_gate = jnp.where(is_live, gate_value, 0.0)
    position = jnp.where(is_live, expert_ids * slot_count + slot_index, expert_count * slot_count)
    owner_table = jnp.full((expert_count * slot_count + 1,), tok_count * choice_count, jnp.int32)
    owner_table = owner_table.at[position.reshape(-1)].set(
        jnp.arange(tok_count * choice_count, dtype=jnp.int32)
    )
    owner_table = owner_table[: expert_count * slot_count]
    zero_row = jnp.zeros((1, width), jnp.bfloat16)
    token_pad = jnp.concatenate([tokens, zero_row], axis=0)
    outgoing = token_pad[owner_table // choice_count].reshape(expert_count, slot_count, width)
    gate_pad = jnp.concatenate([live_gate.reshape(-1), jnp.zeros((1,), jnp.float32)])
    grad_pad = jnp.concatenate([grad_out, zero_row], axis=0)
    grad_rows = (
        gate_pad[owner_table][:, None] * grad_pad[owner_table // choice_count].astype(jnp.float32)
    ).astype(jnp.bfloat16)
    grad_rows = grad_rows.reshape(expert_count, slot_count, width)
    both_in = lax.all_to_all(
        jnp.concatenate([outgoing, grad_rows], axis=1), "expert", split_axis=0, concat_axis=0, tiled=True
    )
    block_shape = (sender_count, local_count, slot_count, width)
    row_block = both_in[:, :slot_count].reshape(block_shape)
    arrived = both_in[:, slot_count:].reshape(block_shape)
    hidden_gate = jnp.einsum(
        "slnd,ldf->slnf", row_block, w_gate, preferred_element_type=jnp.float32
    )
    hidden_up = jnp.einsum(
        "slnd,ldf->slnf", row_block, w_up, preferred_element_type=jnp.float32
    )
    silu_value, silu_slope = silu_parts(hidden_gate)
    activated = (silu_value * hidden_up).astype(jnp.bfloat16)
    expert_out = jnp.einsum(
        "slnf,ldf->slnd", activated, w_down, preferred_element_type=jnp.float32
    ).astype(jnp.bfloat16)
    grad_act = jnp.einsum("slnd,ldf->slnf", arrived, w_down, preferred_element_type=jnp.float32)
    gate_delta = (grad_act * hidden_up * silu_slope).astype(jnp.bfloat16)
    up_delta = (grad_act * silu_value).astype(jnp.bfloat16)
    row_grad = (
        jnp.einsum("slnf,ldf->slnd", gate_delta, w_gate, preferred_element_type=jnp.float32)
        + jnp.einsum("slnf,ldf->slnd", up_delta, w_up, preferred_element_type=jnp.float32)
    ).astype(jnp.bfloat16)
    flat_rows = (sender_count * local_count, slot_count, width)
    both_out = lax.all_to_all(
        jnp.concatenate([expert_out.reshape(flat_rows), row_grad.reshape(flat_rows)], axis=1),
        "expert",
        split_axis=0,
        concat_axis=0,
        tiled=True,
    )
    returned = both_out[:, :slot_count]
    sent_back = both_out[:, slot_count:]
    gate_part = jnp.einsum("slnd,slnf->dlf", row_block, gate_delta, preferred_element_type=jnp.float32)
    up_part = jnp.einsum("slnd,slnf->dlf", row_block, up_delta, preferred_element_type=jnp.float32)
    down_part = jnp.einsum("slnd,slnf->dlf", arrived, activated, preferred_element_type=jnp.float32)
    joined = lax.psum_scatter(
        jnp.concatenate([gate_part, up_part, down_part], axis=2)
        .reshape(lax.axis_size("dp") * own_rows, local_count * 3 * hidden_width)
        .astype(jnp.bfloat16),
        "dp",
        scatter_dimension=0,
        tiled=True,
    ).astype(jnp.float32)
    triple_view = joined.reshape(-1, local_count, 3, hidden_width)
    grad_gate = jnp.transpose(triple_view[:, :, 0, :], (1, 0, 2))
    grad_up = jnp.transpose(triple_view[:, :, 1, :], (1, 0, 2))
    grad_down = jnp.transpose(triple_view[:, :, 2, :], (1, 0, 2))
    out_pad = jnp.concatenate([returned.reshape(-1, width), zero_row], axis=0)
    back_pad = jnp.concatenate([sent_back.reshape(-1, width), zero_row], axis=0)
    dy_wide = grad_out.astype(jnp.float32)
    mixed = jnp.zeros((tok_count, width), jnp.float32)
    row_sum = jnp.zeros((tok_count, width), jnp.float32)
    gate_grads = []
    for which in range(choice_count):
        got_row = out_pad[position[:, which]].astype(jnp.float32)
        mixed = mixed + live_gate[:, which : which + 1] * got_row
        gate_grads.append(jnp.sum(dy_wide * got_row, axis=1))
        row_sum = row_sum + back_pad[position[:, which]].astype(jnp.float32)
    layer_output = mixed.astype(jnp.bfloat16)
    gate_grad = jnp.stack(gate_grads, axis=1)
    cross_term = jnp.sum(gate_grad * gate_value, axis=1, keepdims=True)
    pick_delta = (gate_grad - cross_term) / pick_sum * picked * (1.0 - picked)
    logit_grad = jnp.sum(picker * pick_delta[:, :, None], axis=1)
    grad_tokens = (row_sum + jnp.dot(logit_grad, w_router.T, precision=highest)).astype(
        jnp.bfloat16
    )
    router_part = jnp.dot(tokens_wide.T, logit_grad, precision=highest)
    grad_router = butterfly_sum(butterfly_sum(router_part, "expert"), "dp")
    return (layer_output, grad_tokens, grad_router, grad_gate, grad_up, grad_down)


def solution(mesh):
    return jax.shard_map(
        on_device,
        mesh=mesh,
        in_specs=(
            P(("dp", "expert"), None),
            P(("dp", "expert"), None),
            P(("dp", "expert"), None),
            P(),
            P("expert", None, None),
            P("expert", None, None),
            P("expert", None, None),
            P(("dp", "expert"), None),
        ),
        out_specs=(
            P(("dp", "expert"), None),
            P(("dp", "expert"), None),
            P(),
            P("expert", "dp", None),
            P("expert", "dp", None),
            P("expert", "dp", None),
        ),
        check_vma=False,
    )
```

```python
import jax
import jax.numpy as jnp
from jax import lax
from jax.sharding import PartitionSpec as P


def silu_parts(hidden):
    sigmoid_val = jax.nn.sigmoid(hidden)
    return (hidden * sigmoid_val, sigmoid_val * (1.0 + hidden * (1.0 - sigmoid_val)))


def group_sum(value, axis, low_bit, bits):
    size = lax.axis_size(axis)
    got = [value]
    for offset in range(1, 2**bits):
        step = offset << low_bit
        pairs = [(i, i ^ step) for i in range(size)]
        got.append(lax.ppermute(value, axis, pairs))
    while len(got) > 1:
        got = [got[i] + got[i + 1] for i in range(0, len(got), 2)]
    return got[0]


def all_sum(value, axis):
    size = lax.axis_size(axis)
    low_bit = 0
    while (1 << low_bit) < size:
        bits = min(3, (size - 1).bit_length() - low_bit)
        value = group_sum(value, axis, low_bit, bits)
        low_bit += bits
    return value


def on_device(tokens, expert_ids, slot_index, w_router, w_gate, w_up, w_down, grad_out):
    tok_count, width = tokens.shape
    choice_count = expert_ids.shape[1]
    expert_count = w_router.shape[1]
    local_count = w_gate.shape[0]
    hidden_width = w_gate.shape[2]
    sender_count = lax.axis_size("expert")
    own_rows = width // lax.axis_size("dp")
    slot_count = tok_count * choice_count // expert_count
    highest = lax.Precision.HIGHEST
    tokens_wide = tokens.astype(jnp.float32)
    scores = jax.nn.sigmoid(jnp.dot(tokens_wide, w_router, precision=highest))
    picker = (
        expert_ids[:, :, None] == jnp.arange(expert_count, dtype=jnp.int32)[None, None, :]
    ).astype(jnp.float32)
    picked = jnp.sum(picker * scores[:, None, :], axis=2)
    pick_sum = jnp.sum(picked, axis=1, keepdims=True)
    gate_value = picked / pick_sum
    is_live = slot_index >= 0
    live_gate = jnp.where(is_live, gate_value, 0.0)
    position = jnp.where(is_live, expert_ids * slot_count + slot_index, expert_count * slot_count)
    slot_total = expert_count * slot_count
    chosen = position[:, :, None] == jnp.arange(slot_total, dtype=jnp.int32)[None, None, :]
    slot_of_token = jnp.any(chosen, axis=1)
    gate_of_slot = jnp.sum(jnp.where(chosen, live_gate[:, :, None], 0.0), axis=(0, 1))
    pick_rows = slot_of_token.astype(jnp.bfloat16)
    outgoing = jnp.dot(pick_rows.T, tokens, preferred_element_type=jnp.float32).astype(jnp.bfloat16)
    picked_grad = jnp.dot(pick_rows.T, grad_out, preferred_element_type=jnp.float32)
    grad_rows = (gate_of_slot[:, None] * picked_grad).astype(jnp.bfloat16)
    outgoing = outgoing.reshape(expert_count, slot_count, width)
    grad_rows = grad_rows.reshape(expert_count, slot_count, width)
    both_in = lax.all_to_all(
        jnp.concatenate([outgoing, grad_rows], axis=1), "expert", split_axis=0, concat_axis=0, tiled=True
    )
    block_shape = (sender_count, local_count, slot_count, width)
    row_block = both_in[:, :slot_count].reshape(block_shape)
    arrived = both_in[:, slot_count:].reshape(block_shape)
    hidden_gate = jnp.einsum(
        "slnd,ldf->slnf", row_block, w_gate, preferred_element_type=jnp.float32
    )
    hidden_up = jnp.einsum(
        "slnd,ldf->slnf", row_block, w_up, preferred_element_type=jnp.float32
    )
    silu_value, silu_slope = silu_parts(hidden_gate)
    activated = (silu_value * hidden_up).astype(jnp.bfloat16)
    expert_out = jnp.einsum(
        "slnf,ldf->slnd", activated, w_down, preferred_element_type=jnp.float32
    ).astype(jnp.bfloat16)
    flat_rows = (sender_count * local_count, slot_count, width)
    returned = lax.all_to_all(
        expert_out.reshape(flat_rows), "expert", split_axis=0, concat_axis=0, tiled=True
    )
    grad_act = jnp.einsum("slnd,ldf->slnf", arrived, w_down, preferred_element_type=jnp.float32)
    gate_delta = (grad_act * hidden_up * silu_slope).astype(jnp.bfloat16)
    up_delta = (grad_act * silu_value).astype(jnp.bfloat16)
    row_grad = (
        jnp.einsum("slnf,ldf->slnd", gate_delta, w_gate, preferred_element_type=jnp.float32)
        + jnp.einsum("slnf,ldf->slnd", up_delta, w_up, preferred_element_type=jnp.float32)
    ).astype(jnp.bfloat16)
    sent_back = lax.all_to_all(
        row_grad.reshape(flat_rows), "expert", split_axis=0, concat_axis=0, tiled=True
    )
    gate_part = jnp.einsum("slnd,slnf->dlf", row_block, gate_delta, preferred_element_type=jnp.float32)
    up_part = jnp.einsum("slnd,slnf->dlf", row_block, up_delta, preferred_element_type=jnp.float32)
    down_part = jnp.einsum("slnd,slnf->dlf", arrived, activated, preferred_element_type=jnp.float32)
    joined = lax.psum_scatter(
        jnp.concatenate([gate_part, up_part, down_part], axis=2)
        .reshape(lax.axis_size("dp") * own_rows, local_count * 3 * hidden_width)
        .astype(jnp.bfloat16),
        "dp",
        scatter_dimension=0,
        tiled=True,
    ).astype(jnp.float32)
    triple_view = joined.reshape(-1, local_count, 3, hidden_width)
    grad_gate = jnp.transpose(triple_view[:, :, 0, :], (1, 0, 2))
    grad_up = jnp.transpose(triple_view[:, :, 1, :], (1, 0, 2))
    grad_down = jnp.transpose(triple_view[:, :, 2, :], (1, 0, 2))
    choice_rows = jnp.transpose(chosen, (1, 0, 2)).reshape(choice_count * tok_count, slot_total)
    choice_rows = choice_rows.astype(jnp.bfloat16)
    got_rows = jnp.dot(
        choice_rows, returned.reshape(slot_total, width), preferred_element_type=jnp.float32
    ).reshape(choice_count, tok_count, width)
    back_rows = jnp.dot(
        choice_rows, sent_back.reshape(slot_total, width), preferred_element_type=jnp.float32
    ).reshape(choice_count, tok_count, width)
    dy_wide = grad_out.astype(jnp.float32)
    mixed = jnp.zeros((tok_count, width), jnp.float32)
    row_sum = jnp.zeros((tok_count, width), jnp.float32)
    gate_grads = []
    for which in range(choice_count):
        got_row = got_rows[which]
        mixed = mixed + live_gate[:, which : which + 1] * got_row
        gate_grads.append(jnp.sum(dy_wide * got_row, axis=1))
        row_sum = row_sum + back_rows[which]
    layer_output = mixed.astype(jnp.bfloat16)
    gate_grad = jnp.stack(gate_grads, axis=1)
    cross_term = jnp.sum(gate_grad * gate_value, axis=1, keepdims=True)
    pick_delta = (gate_grad - cross_term) / pick_sum * picked * (1.0 - picked)
    logit_grad = jnp.sum(picker * pick_delta[:, :, None], axis=1)
    grad_tokens = (row_sum + jnp.dot(logit_grad, w_router.T, precision=highest)).astype(
        jnp.bfloat16
    )
    router_part = jnp.dot(tokens_wide.T, logit_grad, precision=highest)
    grad_router = all_sum(all_sum(router_part, "expert"), "dp")
    return (layer_output, grad_tokens, grad_router, grad_gate, grad_up, grad_down)


def solution(mesh):
    return jax.shard_map(
        on_device,
        mesh=mesh,
        in_specs=(
            P(("dp", "expert"), None),
            P(("dp", "expert"), None),
            P(("dp", "expert"), None),
            P(),
            P("expert", None, None),
            P("expert", None, None),
            P("expert", None, None),
            P(("dp", "expert"), None),
        ),
        out_specs=(
            P(("dp", "expert"), None),
            P(("dp", "expert"), None),
            P(),
            P("expert", "dp", None),
            P("expert", "dp", None),
            P("expert", "dp", None),
        ),
        check_vma=False,
    )
```

```python
import jax
import jax.numpy as jnp
from jax import lax
from jax.sharding import PartitionSpec as P


def silu_parts(hidden):
    sigmoid_val = jax.nn.sigmoid(hidden)
    return (hidden * sigmoid_val, sigmoid_val * (1.0 + hidden * (1.0 - sigmoid_val)))


def group_sum(value, axis, low_bit, bits):
    size = lax.axis_size(axis)
    got = [value]
    for offset in range(1, 2**bits):
        step = offset << low_bit
        pairs = [(i, i ^ step) for i in range(size)]
        got.append(lax.ppermute(value, axis, pairs))
    while len(got) > 1:
        got = [got[i] + got[i + 1] for i in range(0, len(got), 2)]
    return got[0]


def all_sum(value, axis):
    size = lax.axis_size(axis)
    low_bit = 0
    while (1 << low_bit) < size:
        bits = min(3, (size - 1).bit_length() - low_bit)
        value = group_sum(value, axis, low_bit, bits)
        low_bit += bits
    return value


def on_device(tokens, expert_ids, slot_index, w_router, w_gate, w_up, w_down, grad_out):
    tok_count, width = tokens.shape
    choice_count = expert_ids.shape[1]
    expert_count = w_router.shape[1]
    local_count = w_gate.shape[0]
    hidden_width = w_gate.shape[2]
    sender_count = lax.axis_size("expert")
    own_rows = width // lax.axis_size("dp")
    slot_count = tok_count * choice_count // expert_count
    highest = lax.Precision.HIGHEST
    tokens_wide = tokens.astype(jnp.float32)
    scores = jax.nn.sigmoid(jnp.dot(tokens_wide, w_router, precision=highest))
    picker = (
        expert_ids[:, :, None] == jnp.arange(expert_count, dtype=jnp.int32)[None, None, :]
    ).astype(jnp.float32)
    picked = jnp.sum(picker * scores[:, None, :], axis=2)
    pick_sum = jnp.sum(picked, axis=1, keepdims=True)
    gate_value = picked / pick_sum
    is_live = slot_index >= 0
    live_gate = jnp.where(is_live, gate_value, 0.0)
    position = jnp.where(is_live, expert_ids * slot_count + slot_index, expert_count * slot_count)
    slot_total = expert_count * slot_count
    chosen = position[:, :, None] == jnp.arange(slot_total, dtype=jnp.int32)[None, None, :]
    slot_of_token = jnp.any(chosen, axis=1)
    gate_of_slot = jnp.sum(jnp.where(chosen, live_gate[:, :, None], 0.0), axis=(0, 1))
    pick_rows = slot_of_token.astype(jnp.bfloat16)
    outgoing = jnp.dot(pick_rows.T, tokens, preferred_element_type=jnp.float32).astype(jnp.bfloat16)
    picked_grad = jnp.dot(pick_rows.T, grad_out, preferred_element_type=jnp.float32)
    grad_rows = (gate_of_slot[:, None] * picked_grad).astype(jnp.bfloat16)
    outgoing = outgoing.reshape(expert_count, slot_count, width)
    grad_rows = grad_rows.reshape(expert_count, slot_count, width)
    both_in = lax.all_to_all(
        jnp.concatenate([outgoing, grad_rows], axis=1), "expert", split_axis=0, concat_axis=0, tiled=True
    )
    block_shape = (sender_count, local_count, slot_count, width)
    row_block = both_in[:, :slot_count].reshape(block_shape)
    arrived = both_in[:, slot_count:].reshape(block_shape)
    hidden_gate = jnp.einsum(
        "slnd,ldf->slnf", row_block, w_gate, preferred_element_type=jnp.float32
    )
    hidden_up = jnp.einsum(
        "slnd,ldf->slnf", row_block, w_up, preferred_element_type=jnp.float32
    )
    silu_value, silu_slope = silu_parts(hidden_gate)
    activated = (silu_value * hidden_up).astype(jnp.bfloat16)
    expert_out = jnp.einsum(
        "slnf,ldf->slnd", activated, w_down, preferred_element_type=jnp.float32
    ).astype(jnp.bfloat16)
    flat_rows = (sender_count * local_count, slot_count, width)
    returned = lax.all_to_all(
        expert_out.reshape(flat_rows), "expert", split_axis=0, concat_axis=0, tiled=True
    )
    grad_act = jnp.einsum("slnd,ldf->slnf", arrived, w_down, preferred_element_type=jnp.float32)
    gate_delta = (grad_act * hidden_up * silu_slope).astype(jnp.bfloat16)
    up_delta = (grad_act * silu_value).astype(jnp.bfloat16)
    row_grad = (
        jnp.einsum("slnf,ldf->slnd", gate_delta, w_gate, preferred_element_type=jnp.float32)
        + jnp.einsum("slnf,ldf->slnd", up_delta, w_up, preferred_element_type=jnp.float32)
    ).astype(jnp.bfloat16)
    sent_back = lax.all_to_all(
        row_grad.reshape(flat_rows), "expert", split_axis=0, concat_axis=0, tiled=True
    )
    gate_part = jnp.einsum("slnd,slnf->dlf", row_block, gate_delta, preferred_element_type=jnp.float32)
    up_part = jnp.einsum("slnd,slnf->dlf", row_block, up_delta, preferred_element_type=jnp.float32)
    down_part = jnp.einsum("slnd,slnf->dlf", arrived, activated, preferred_element_type=jnp.float32)
    joined = lax.psum_scatter(
        jnp.concatenate([gate_part, up_part, down_part], axis=2)
        .reshape(lax.axis_size("dp") * own_rows, local_count * 3 * hidden_width)
        .astype(jnp.bfloat16),
        "dp",
        scatter_dimension=0,
        tiled=True,
    ).astype(jnp.float32)
    triple_view = joined.reshape(-1, local_count, 3, hidden_width)
    grad_gate = jnp.transpose(triple_view[:, :, 0, :], (1, 0, 2))
    grad_up = jnp.transpose(triple_view[:, :, 1, :], (1, 0, 2))
    grad_down = jnp.transpose(triple_view[:, :, 2, :], (1, 0, 2))
    choice_rows = jnp.transpose(chosen, (1, 0, 2)).reshape(choice_count * tok_count, slot_total)
    choice_rows = choice_rows.astype(jnp.bfloat16)
    got_rows = jnp.dot(
        choice_rows, returned.reshape(slot_total, width), preferred_element_type=jnp.float32
    ).reshape(choice_count, tok_count, width)
    back_rows = jnp.dot(
        choice_rows, sent_back.reshape(slot_total, width), preferred_element_type=jnp.float32
    ).reshape(choice_count, tok_count, width)
    dy_wide = grad_out.astype(jnp.float32)
    mixed = jnp.zeros((tok_count, width), jnp.float32)
    row_sum = jnp.zeros((tok_count, width), jnp.float32)
    gate_grads = []
    for which in range(choice_count):
        got_row = got_rows[which]
        mixed = mixed + live_gate[:, which : which + 1] * got_row
        gate_grads.append(jnp.sum(dy_wide * got_row, axis=1))
        row_sum = row_sum + back_rows[which]
    layer_output = mixed.astype(jnp.bfloat16)
    gate_grad = jnp.stack(gate_grads, axis=1)
    cross_term = jnp.sum(gate_grad * gate_value, axis=1, keepdims=True)
    pick_delta = (gate_grad - cross_term) / pick_sum * picked * (1.0 - picked)
    logit_grad = jnp.sum(picker * pick_delta[:, :, None], axis=1)
    grad_tokens = (row_sum + jnp.dot(logit_grad, w_router.T, precision=highest)).astype(
        jnp.bfloat16
    )
    router_part = jnp.dot(tokens_wide.T, logit_grad, precision=highest)
    grad_router = all_sum(all_sum(router_part, "dp"), "expert")
    return (layer_output, grad_tokens, grad_router, grad_gate, grad_up, grad_down)


def solution(mesh):
    return jax.shard_map(
        on_device,
        mesh=mesh,
        in_specs=(
            P(("dp", "expert"), None),
            P(("dp", "expert"), None),
            P(("dp", "expert"), None),
            P(),
            P("expert", None, None),
            P("expert", None, None),
            P("expert", None, None),
            P(("dp", "expert"), None),
        ),
        out_specs=(
            P(("dp", "expert"), None),
            P(("dp", "expert"), None),
            P(),
            P("expert", "dp", None),
            P("expert", "dp", None),
            P("expert", "dp", None),
        ),
        check_vma=False,
    )
```

```python
import jax
import jax.numpy as jnp
from jax import lax
from jax.sharding import PartitionSpec as P
from jax.experimental import pallas as pl


def silu_parts(hidden):
    sigmoid_val = jax.nn.sigmoid(hidden)
    return (hidden * sigmoid_val, sigmoid_val * (1.0 + hidden * (1.0 - sigmoid_val)))


def group_sum(value, axis, low_bit, bits):
    size = lax.axis_size(axis)
    got = [value]
    for offset in range(1, 2**bits):
        step = offset << low_bit
        pairs = [(i, i ^ step) for i in range(size)]
        got.append(lax.ppermute(value, axis, pairs))
    while len(got) > 1:
        got = [got[i] + got[i + 1] for i in range(0, len(got), 2)]
    return got[0]


def all_sum(value, axis):
    size = lax.axis_size(axis)
    low_bit = 0
    while (1 << low_bit) < size:
        bits = min(3, (size - 1).bit_length() - low_bit)
        value = group_sum(value, axis, low_bit, bits)
        low_bit += bits
    return value


def weight_grad_kernel(rows_t_ref, grads_t_ref, deltas_ref, act_ref, out_ref):
    split = deltas_ref.shape[1]
    both = jnp.dot(rows_t_ref[...], deltas_ref[...], preferred_element_type=jnp.float32)
    down = jnp.dot(grads_t_ref[...], act_ref[...], preferred_element_type=jnp.float32)
    out_ref[:, :split] = both.astype(out_ref.dtype)
    out_ref[:, split:] = down.astype(out_ref.dtype)


def weight_grads(rows, grads, gate_delta, up_delta, activated):
    width = rows.shape[1]
    count = rows.shape[0]
    hidden = activated.shape[1]
    deltas = jnp.concatenate([gate_delta, up_delta], axis=1)
    tile = 256
    return pl.pallas_call(
        weight_grad_kernel,
        grid=(width // tile,),
        in_specs=[
            pl.BlockSpec((tile, count), lambda i: (i, 0)),
            pl.BlockSpec((tile, count), lambda i: (i, 0)),
            pl.BlockSpec((count, 2 * hidden), lambda i: (0, 0)),
            pl.BlockSpec((count, hidden), lambda i: (0, 0)),
        ],
        out_specs=pl.BlockSpec((tile, 3 * hidden), lambda i: (i, 0)),
        out_shape=jax.ShapeDtypeStruct((width, 3 * hidden), jnp.bfloat16),
    )(rows.T, grads.T, deltas, activated)


def on_device(tokens, expert_ids, slot_index, w_router, w_gate, w_up, w_down, grad_out):
    tok_count, width = tokens.shape
    choice_count = expert_ids.shape[1]
    expert_count = w_router.shape[1]
    local_count = w_gate.shape[0]
    hidden_width = w_gate.shape[2]
    sender_count = lax.axis_size("expert")
    own_rows = width // lax.axis_size("dp")
    slot_count = tok_count * choice_count // expert_count
    highest = lax.Precision.HIGHEST
    tokens_wide = tokens.astype(jnp.float32)
    scores = jax.nn.sigmoid(jnp.dot(tokens_wide, w_router, precision=highest))
    picker = (
        expert_ids[:, :, None] == jnp.arange(expert_count, dtype=jnp.int32)[None, None, :]
    ).astype(jnp.float32)
    picked = jnp.sum(picker * scores[:, None, :], axis=2)
    pick_sum = jnp.sum(picked, axis=1, keepdims=True)
    gate_value = picked / pick_sum
    is_live = slot_index >= 0
    live_gate = jnp.where(is_live, gate_value, 0.0)
    position = jnp.where(is_live, expert_ids * slot_count + slot_index, expert_count * slot_count)
    slot_total = expert_count * slot_count
    chosen = position[:, :, None] == jnp.arange(slot_total, dtype=jnp.int32)[None, None, :]
    slot_of_token = jnp.any(chosen, axis=1)
    gate_of_slot = jnp.sum(jnp.where(chosen, live_gate[:, :, None], 0.0), axis=(0, 1))
    pick_rows = slot_of_token.astype(jnp.bfloat16)
    outgoing = jnp.dot(pick_rows.T, tokens, preferred_element_type=jnp.float32).astype(jnp.bfloat16)
    picked_grad = jnp.dot(pick_rows.T, grad_out, preferred_element_type=jnp.float32)
    grad_rows = (gate_of_slot[:, None] * picked_grad).astype(jnp.bfloat16)
    outgoing = outgoing.reshape(expert_count, slot_count, width)
    grad_rows = grad_rows.reshape(expert_count, slot_count, width)
    both_in = lax.all_to_all(
        jnp.concatenate([outgoing, grad_rows], axis=1), "expert", split_axis=0, concat_axis=0, tiled=True
    )
    block_shape = (sender_count, local_count, slot_count, width)
    row_block = both_in[:, :slot_count].reshape(block_shape)
    arrived = both_in[:, slot_count:].reshape(block_shape)
    hidden_gate = jnp.einsum(
        "slnd,ldf->slnf", row_block, w_gate, preferred_element_type=jnp.float32
    )
    hidden_up = jnp.einsum(
        "slnd,ldf->slnf", row_block, w_up, preferred_element_type=jnp.float32
    )
    silu_value, silu_slope = silu_parts(hidden_gate)
    activated = (silu_value * hidden_up).astype(jnp.bfloat16)
    expert_out = jnp.einsum(
        "slnf,ldf->slnd", activated, w_down, preferred_element_type=jnp.float32
    ).astype(jnp.bfloat16)
    flat_rows = (sender_count * local_count, slot_count, width)
    returned = lax.all_to_all(
        expert_out.reshape(flat_rows), "expert", split_axis=0, concat_axis=0, tiled=True
    )
    grad_act = jnp.einsum("slnd,ldf->slnf", arrived, w_down, preferred_element_type=jnp.float32)
    gate_delta = (grad_act * hidden_up * silu_slope).astype(jnp.bfloat16)
    up_delta = (grad_act * silu_value).astype(jnp.bfloat16)
    row_grad = (
        jnp.einsum("slnf,ldf->slnd", gate_delta, w_gate, preferred_element_type=jnp.float32)
        + jnp.einsum("slnf,ldf->slnd", up_delta, w_up, preferred_element_type=jnp.float32)
    ).astype(jnp.bfloat16)
    sent_back = lax.all_to_all(
        row_grad.reshape(flat_rows), "expert", split_axis=0, concat_axis=0, tiled=True
    )
    if local_count == 1:
        flat = (sender_count * slot_count, -1)
        partials = weight_grads(
            row_block.reshape(flat),
            arrived.reshape(flat),
            gate_delta.reshape(flat),
            up_delta.reshape(flat),
            activated.reshape(flat),
        )
    else:
        gate_part = jnp.einsum("slnd,slnf->dlf", row_block, gate_delta, preferred_element_type=jnp.float32)
        up_part = jnp.einsum("slnd,slnf->dlf", row_block, up_delta, preferred_element_type=jnp.float32)
        down_part = jnp.einsum("slnd,slnf->dlf", arrived, activated, preferred_element_type=jnp.float32)
        partials = (
            jnp.concatenate([gate_part, up_part, down_part], axis=2)
            .reshape(lax.axis_size("dp") * own_rows, local_count * 3 * hidden_width)
            .astype(jnp.bfloat16)
        )
    joined = lax.psum_scatter(partials, "dp", scatter_dimension=0, tiled=True).astype(jnp.float32)
    triple_view = joined.reshape(-1, local_count, 3, hidden_width)
    grad_gate = jnp.transpose(triple_view[:, :, 0, :], (1, 0, 2))
    grad_up = jnp.transpose(triple_view[:, :, 1, :], (1, 0, 2))
    grad_down = jnp.transpose(triple_view[:, :, 2, :], (1, 0, 2))
    choice_rows = jnp.transpose(chosen, (1, 0, 2)).reshape(choice_count * tok_count, slot_total)
    choice_rows = choice_rows.astype(jnp.bfloat16)
    got_rows = jnp.dot(
        choice_rows, returned.reshape(slot_total, width), preferred_element_type=jnp.float32
    ).reshape(choice_count, tok_count, width)
    back_rows = jnp.dot(
        choice_rows, sent_back.reshape(slot_total, width), preferred_element_type=jnp.float32
    ).reshape(choice_count, tok_count, width)
    dy_wide = grad_out.astype(jnp.float32)
    mixed = jnp.zeros((tok_count, width), jnp.float32)
    row_sum = jnp.zeros((tok_count, width), jnp.float32)
    gate_grads = []
    for which in range(choice_count):
        got_row = got_rows[which]
        mixed = mixed + live_gate[:, which : which + 1] * got_row
        gate_grads.append(jnp.sum(dy_wide * got_row, axis=1))
        row_sum = row_sum + back_rows[which]
    layer_output = mixed.astype(jnp.bfloat16)
    gate_grad = jnp.stack(gate_grads, axis=1)
    cross_term = jnp.sum(gate_grad * gate_value, axis=1, keepdims=True)
    pick_delta = (gate_grad - cross_term) / pick_sum * picked * (1.0 - picked)
    logit_grad = jnp.sum(picker * pick_delta[:, :, None], axis=1)
    grad_tokens = (row_sum + jnp.dot(logit_grad, w_router.T, precision=highest)).astype(
        jnp.bfloat16
    )
    router_part = jnp.dot(tokens_wide.T, logit_grad, precision=highest)
    grad_router = all_sum(all_sum(router_part, "dp"), "expert")
    return (layer_output, grad_tokens, grad_router, grad_gate, grad_up, grad_down)


def solution(mesh):
    return jax.shard_map(
        on_device,
        mesh=mesh,
        in_specs=(
            P(("dp", "expert"), None),
            P(("dp", "expert"), None),
            P(("dp", "expert"), None),
            P(),
            P("expert", None, None),
            P("expert", None, None),
            P("expert", None, None),
            P(("dp", "expert"), None),
        ),
        out_specs=(
            P(("dp", "expert"), None),
            P(("dp", "expert"), None),
            P(),
            P("expert", "dp", None),
            P("expert", "dp", None),
            P("expert", "dp", None),
        ),
        check_vma=False,
    )
```

```python
import jax
import jax.numpy as jnp
from jax import lax
from jax.sharding import PartitionSpec as P
from jax.experimental import pallas as pl


def silu_parts(hidden):
    sigmoid_val = jax.nn.sigmoid(hidden)
    return (hidden * sigmoid_val, sigmoid_val * (1.0 + hidden * (1.0 - sigmoid_val)))


def group_sum(value, axis, low_bit, bits):
    size = lax.axis_size(axis)
    got = [value]
    for offset in range(1, 2**bits):
        step = offset << low_bit
        pairs = [(i, i ^ step) for i in range(size)]
        got.append(lax.ppermute(value, axis, pairs))
    while len(got) > 1:
        got = [got[i] + got[i + 1] for i in range(0, len(got), 2)]
    return got[0]


def all_sum(value, axis):
    size = lax.axis_size(axis)
    low_bit = 0
    while (1 << low_bit) < size:
        bits = min(3, (size - 1).bit_length() - low_bit)
        value = group_sum(value, axis, low_bit, bits)
        low_bit += bits
    return value


def weight_grad_kernel(rows_ref, grads_ref, deltas_ref, act_ref, out_ref):
    split = deltas_ref.shape[1]
    inner = (((0,), (0,)), ((), ()))
    both = lax.dot_general(rows_ref[...], deltas_ref[...], inner, preferred_element_type=jnp.float32)
    down = lax.dot_general(grads_ref[...], act_ref[...], inner, preferred_element_type=jnp.float32)
    out_ref[:, :split] = both.astype(out_ref.dtype)
    out_ref[:, split:] = down.astype(out_ref.dtype)


def weight_grads(rows, grads, gate_delta, up_delta, activated):
    width = rows.shape[1]
    count = rows.shape[0]
    hidden = activated.shape[1]
    deltas = jnp.concatenate([gate_delta, up_delta], axis=1)
    tile = 512
    return pl.pallas_call(
        weight_grad_kernel,
        grid=(width // tile,),
        in_specs=[
            pl.BlockSpec((count, tile), lambda i: (0, i)),
            pl.BlockSpec((count, tile), lambda i: (0, i)),
            pl.BlockSpec((count, 2 * hidden), lambda i: (0, 0)),
            pl.BlockSpec((count, hidden), lambda i: (0, 0)),
        ],
        out_specs=pl.BlockSpec((tile, 3 * hidden), lambda i: (i, 0)),
        out_shape=jax.ShapeDtypeStruct((width, 3 * hidden), jnp.bfloat16),
    )(rows, grads, deltas, activated)


def on_device(tokens, expert_ids, slot_index, w_router, w_gate, w_up, w_down, grad_out):
    tok_count, width = tokens.shape
    choice_count = expert_ids.shape[1]
    expert_count = w_router.shape[1]
    local_count = w_gate.shape[0]
    hidden_width = w_gate.shape[2]
    sender_count = lax.axis_size("expert")
    own_rows = width // lax.axis_size("dp")
    slot_count = tok_count * choice_count // expert_count
    highest = lax.Precision.HIGHEST
    tokens_wide = tokens.astype(jnp.float32)
    scores = jax.nn.sigmoid(jnp.dot(tokens_wide, w_router, precision=highest))
    picker = (
        expert_ids[:, :, None] == jnp.arange(expert_count, dtype=jnp.int32)[None, None, :]
    ).astype(jnp.float32)
    picked = jnp.sum(picker * scores[:, None, :], axis=2)
    pick_sum = jnp.sum(picked, axis=1, keepdims=True)
    gate_value = picked / pick_sum
    is_live = slot_index >= 0
    live_gate = jnp.where(is_live, gate_value, 0.0)
    position = jnp.where(is_live, expert_ids * slot_count + slot_index, expert_count * slot_count)
    slot_total = expert_count * slot_count
    chosen = position[:, :, None] == jnp.arange(slot_total, dtype=jnp.int32)[None, None, :]
    slot_of_token = jnp.any(chosen, axis=1)
    gate_of_slot = jnp.sum(jnp.where(chosen, live_gate[:, :, None], 0.0), axis=(0, 1))
    pick_rows = slot_of_token.astype(jnp.bfloat16)
    outgoing = jnp.dot(pick_rows.T, tokens, preferred_element_type=jnp.float32).astype(jnp.bfloat16)
    picked_grad = jnp.dot(pick_rows.T, grad_out, preferred_element_type=jnp.float32)
    grad_rows = (gate_of_slot[:, None] * picked_grad).astype(jnp.bfloat16)
    outgoing = outgoing.reshape(expert_count, slot_count, width)
    grad_rows = grad_rows.reshape(expert_count, slot_count, width)
    both_in = lax.all_to_all(
        jnp.concatenate([outgoing, grad_rows], axis=1), "expert", split_axis=0, concat_axis=0, tiled=True
    )
    block_shape = (sender_count, local_count, slot_count, width)
    row_block = both_in[:, :slot_count].reshape(block_shape)
    arrived = both_in[:, slot_count:].reshape(block_shape)
    hidden_gate = jnp.einsum(
        "slnd,ldf->slnf", row_block, w_gate, preferred_element_type=jnp.float32
    )
    hidden_up = jnp.einsum(
        "slnd,ldf->slnf", row_block, w_up, preferred_element_type=jnp.float32
    )
    silu_value, silu_slope = silu_parts(hidden_gate)
    activated = (silu_value * hidden_up).astype(jnp.bfloat16)
    expert_out = jnp.einsum(
        "slnf,ldf->slnd", activated, w_down, preferred_element_type=jnp.float32
    ).astype(jnp.bfloat16)
    flat_rows = (sender_count * local_count, slot_count, width)
    returned = lax.all_to_all(
        expert_out.reshape(flat_rows), "expert", split_axis=0, concat_axis=0, tiled=True
    )
    grad_act = jnp.einsum("slnd,ldf->slnf", arrived, w_down, preferred_element_type=jnp.float32)
    gate_delta = (grad_act * hidden_up * silu_slope).astype(jnp.bfloat16)
    up_delta = (grad_act * silu_value).astype(jnp.bfloat16)
    row_grad = (
        jnp.einsum("slnf,ldf->slnd", gate_delta, w_gate, preferred_element_type=jnp.float32)
        + jnp.einsum("slnf,ldf->slnd", up_delta, w_up, preferred_element_type=jnp.float32)
    ).astype(jnp.bfloat16)
    sent_back = lax.all_to_all(
        row_grad.reshape(flat_rows), "expert", split_axis=0, concat_axis=0, tiled=True
    )
    if local_count == 1:
        flat = (sender_count * slot_count, -1)
        partials = weight_grads(
            row_block.reshape(flat),
            arrived.reshape(flat),
            gate_delta.reshape(flat),
            up_delta.reshape(flat),
            activated.reshape(flat),
        )
    else:
        gate_part = jnp.einsum("slnd,slnf->dlf", row_block, gate_delta, preferred_element_type=jnp.float32)
        up_part = jnp.einsum("slnd,slnf->dlf", row_block, up_delta, preferred_element_type=jnp.float32)
        down_part = jnp.einsum("slnd,slnf->dlf", arrived, activated, preferred_element_type=jnp.float32)
        partials = (
            jnp.concatenate([gate_part, up_part, down_part], axis=2)
            .reshape(lax.axis_size("dp") * own_rows, local_count * 3 * hidden_width)
            .astype(jnp.bfloat16)
        )
    joined = lax.psum_scatter(partials, "dp", scatter_dimension=0, tiled=True).astype(jnp.float32)
    triple_view = joined.reshape(-1, local_count, 3, hidden_width)
    grad_gate = jnp.transpose(triple_view[:, :, 0, :], (1, 0, 2))
    grad_up = jnp.transpose(triple_view[:, :, 1, :], (1, 0, 2))
    grad_down = jnp.transpose(triple_view[:, :, 2, :], (1, 0, 2))
    choice_rows = jnp.transpose(chosen, (1, 0, 2)).reshape(choice_count * tok_count, slot_total)
    choice_rows = choice_rows.astype(jnp.bfloat16)
    got_rows = jnp.dot(
        choice_rows, returned.reshape(slot_total, width), preferred_element_type=jnp.float32
    ).reshape(choice_count, tok_count, width)
    back_rows = jnp.dot(
        choice_rows, sent_back.reshape(slot_total, width), preferred_element_type=jnp.float32
    ).reshape(choice_count, tok_count, width)
    dy_wide = grad_out.astype(jnp.float32)
    mixed = jnp.zeros((tok_count, width), jnp.float32)
    row_sum = jnp.zeros((tok_count, width), jnp.float32)
    gate_grads = []
    for which in range(choice_count):
        got_row = got_rows[which]
        mixed = mixed + live_gate[:, which : which + 1] * got_row
        gate_grads.append(jnp.sum(dy_wide * got_row, axis=1))
        row_sum = row_sum + back_rows[which]
    layer_output = mixed.astype(jnp.bfloat16)
    gate_grad = jnp.stack(gate_grads, axis=1)
    cross_term = jnp.sum(gate_grad * gate_value, axis=1, keepdims=True)
    pick_delta = (gate_grad - cross_term) / pick_sum * picked * (1.0 - picked)
    logit_grad = jnp.sum(picker * pick_delta[:, :, None], axis=1)
    grad_tokens = (row_sum + jnp.dot(logit_grad, w_router.T, precision=highest)).astype(
        jnp.bfloat16
    )
    router_part = jnp.dot(tokens_wide.T, logit_grad, precision=highest)
    grad_router = all_sum(all_sum(router_part, "dp"), "expert")
    return (layer_output, grad_tokens, grad_router, grad_gate, grad_up, grad_down)


def solution(mesh):
    return jax.shard_map(
        on_device,
        mesh=mesh,
        in_specs=(
            P(("dp", "expert"), None),
            P(("dp", "expert"), None),
            P(("dp", "expert"), None),
            P(),
            P("expert", None, None),
            P("expert", None, None),
            P("expert", None, None),
            P(("dp", "expert"), None),
        ),
        out_specs=(
            P(("dp", "expert"), None),
            P(("dp", "expert"), None),
            P(),
            P("expert", "dp", None),
            P("expert", "dp", None),
            P("expert", "dp", None),
        ),
        check_vma=False,
    )
```

```python
import jax
import jax.numpy as jnp
from jax import lax
from jax.sharding import PartitionSpec as P
from jax.experimental import pallas as pl


def silu_parts(hidden):
    sigmoid_val = jax.nn.sigmoid(hidden)
    return (hidden * sigmoid_val, sigmoid_val * (1.0 + hidden * (1.0 - sigmoid_val)))


def group_sum(value, axis, low_bit, bits):
    size = lax.axis_size(axis)
    got = [value]
    for offset in range(1, 2**bits):
        step = offset << low_bit
        pairs = [(i, i ^ step) for i in range(size)]
        got.append(lax.ppermute(value, axis, pairs))
    while len(got) > 1:
        got = [got[i] + got[i + 1] for i in range(0, len(got), 2)]
    return got[0]


def all_sum(value, axis):
    size = lax.axis_size(axis)
    low_bit = 0
    while (1 << low_bit) < size:
        bits = min(3, (size - 1).bit_length() - low_bit)
        value = group_sum(value, axis, low_bit, bits)
        low_bit += bits
    return value


def outer_kernel(rows_ref, deltas_ref, out_ref):
    inner = (((0,), (0,)), ((), ()))
    out_ref[...] = lax.dot_general(
        rows_ref[...], deltas_ref[...], inner, preferred_element_type=jnp.float32
    ).astype(out_ref.dtype)


def outer_bf16(rows, deltas):
    count, width = rows.shape
    cols = deltas.shape[1]
    tile = 512
    return pl.pallas_call(
        outer_kernel,
        grid=(width // tile,),
        in_specs=[
            pl.BlockSpec((count, tile), lambda i: (0, i)),
            pl.BlockSpec((count, cols), lambda i: (0, 0)),
        ],
        out_specs=pl.BlockSpec((tile, cols), lambda i: (i, 0)),
        out_shape=jax.ShapeDtypeStruct((width, cols), jnp.bfloat16),
    )(rows, deltas)


def on_device(tokens, expert_ids, slot_index, w_router, w_gate, w_up, w_down, grad_out):
    tok_count, width = tokens.shape
    choice_count = expert_ids.shape[1]
    expert_count = w_router.shape[1]
    local_count = w_gate.shape[0]
    hidden_width = w_gate.shape[2]
    sender_count = lax.axis_size("expert")
    own_rows = width // lax.axis_size("dp")
    slot_count = tok_count * choice_count // expert_count
    highest = lax.Precision.HIGHEST
    tokens_wide = tokens.astype(jnp.float32)
    scores = jax.nn.sigmoid(jnp.dot(tokens_wide, w_router, precision=highest))
    picker = (
        expert_ids[:, :, None] == jnp.arange(expert_count, dtype=jnp.int32)[None, None, :]
    ).astype(jnp.float32)
    picked = jnp.sum(picker * scores[:, None, :], axis=2)
    pick_sum = jnp.sum(picked, axis=1, keepdims=True)
    gate_value = picked / pick_sum
    is_live = slot_index >= 0
    live_gate = jnp.where(is_live, gate_value, 0.0)
    position = jnp.where(is_live, expert_ids * slot_count + slot_index, expert_count * slot_count)
    slot_total = expert_count * slot_count
    chosen = position[:, :, None] == jnp.arange(slot_total, dtype=jnp.int32)[None, None, :]
    slot_of_token = jnp.any(chosen, axis=1)
    gate_of_slot = jnp.sum(jnp.where(chosen, live_gate[:, :, None], 0.0), axis=(0, 1))
    pick_rows = slot_of_token.astype(jnp.bfloat16)
    outgoing = jnp.dot(pick_rows.T, tokens, preferred_element_type=jnp.float32).astype(jnp.bfloat16)
    picked_grad = jnp.dot(pick_rows.T, grad_out, preferred_element_type=jnp.float32)
    grad_rows = (gate_of_slot[:, None] * picked_grad).astype(jnp.bfloat16)
    outgoing = outgoing.reshape(expert_count, slot_count, width)
    grad_rows = grad_rows.reshape(expert_count, slot_count, width)
    both_in = lax.all_to_all(
        jnp.concatenate([outgoing, grad_rows], axis=1), "expert", split_axis=0, concat_axis=0, tiled=True
    )
    block_shape = (sender_count, local_count, slot_count, width)
    row_block = both_in[:, :slot_count].reshape(block_shape)
    arrived = both_in[:, slot_count:].reshape(block_shape)
    hidden_gate = jnp.einsum(
        "slnd,ldf->slnf", row_block, w_gate, preferred_element_type=jnp.float32
    )
    hidden_up = jnp.einsum(
        "slnd,ldf->slnf", row_block, w_up, preferred_element_type=jnp.float32
    )
    silu_value, silu_slope = silu_parts(hidden_gate)
    activated = (silu_value * hidden_up).astype(jnp.bfloat16)
    expert_out = jnp.einsum(
        "slnf,ldf->slnd", activated, w_down, preferred_element_type=jnp.float32
    ).astype(jnp.bfloat16)
    flat_rows = (sender_count * local_count, slot_count, width)
    returned = lax.all_to_all(
        expert_out.reshape(flat_rows), "expert", split_axis=0, concat_axis=0, tiled=True
    )
    grad_act = jnp.einsum("slnd,ldf->slnf", arrived, w_down, preferred_element_type=jnp.float32)
    gate_delta = (grad_act * hidden_up * silu_slope).astype(jnp.bfloat16)
    up_delta = (grad_act * silu_value).astype(jnp.bfloat16)
    row_grad = (
        jnp.einsum("slnf,ldf->slnd", gate_delta, w_gate, preferred_element_type=jnp.float32)
        + jnp.einsum("slnf,ldf->slnd", up_delta, w_up, preferred_element_type=jnp.float32)
    ).astype(jnp.bfloat16)
    sent_back = lax.all_to_all(
        row_grad.reshape(flat_rows), "expert", split_axis=0, concat_axis=0, tiled=True
    )
    if local_count == 1:
        flat = (sender_count * slot_count, -1)
        down_sum = lax.psum_scatter(
            outer_bf16(arrived.reshape(flat), activated.reshape(flat)), "dp", scatter_dimension=0, tiled=True
        ).astype(jnp.float32)
        deltas = jnp.concatenate([gate_delta.reshape(flat), up_delta.reshape(flat)], axis=1)
        gate_up_sum = lax.psum_scatter(
            outer_bf16(row_block.reshape(flat), deltas), "dp", scatter_dimension=0, tiled=True
        ).astype(jnp.float32)
        grad_gate = gate_up_sum[None, :, :hidden_width]
        grad_up = gate_up_sum[None, :, hidden_width:]
        grad_down = down_sum[None]
    else:
        gate_part = jnp.einsum("slnd,slnf->dlf", row_block, gate_delta, preferred_element_type=jnp.float32)
        up_part = jnp.einsum("slnd,slnf->dlf", row_block, up_delta, preferred_element_type=jnp.float32)
        down_part = jnp.einsum("slnd,slnf->dlf", arrived, activated, preferred_element_type=jnp.float32)
        partials = (
            jnp.concatenate([gate_part, up_part, down_part], axis=2)
            .reshape(lax.axis_size("dp") * own_rows, local_count * 3 * hidden_width)
            .astype(jnp.bfloat16)
        )
        joined = lax.psum_scatter(partials, "dp", scatter_dimension=0, tiled=True).astype(jnp.float32)
        triple_view = joined.reshape(-1, local_count, 3, hidden_width)
        grad_gate = jnp.transpose(triple_view[:, :, 0, :], (1, 0, 2))
        grad_up = jnp.transpose(triple_view[:, :, 1, :], (1, 0, 2))
        grad_down = jnp.transpose(triple_view[:, :, 2, :], (1, 0, 2))
    choice_rows = jnp.transpose(chosen, (1, 0, 2)).reshape(choice_count * tok_count, slot_total)
    choice_rows = choice_rows.astype(jnp.bfloat16)
    got_rows = jnp.dot(
        choice_rows, returned.reshape(slot_total, width), preferred_element_type=jnp.float32
    ).reshape(choice_count, tok_count, width)
    back_rows = jnp.dot(
        choice_rows, sent_back.reshape(slot_total, width), preferred_element_type=jnp.float32
    ).reshape(choice_count, tok_count, width)
    dy_wide = grad_out.astype(jnp.float32)
    mixed = jnp.zeros((tok_count, width), jnp.float32)
    row_sum = jnp.zeros((tok_count, width), jnp.float32)
    gate_grads = []
    for which in range(choice_count):
        got_row = got_rows[which]
        mixed = mixed + live_gate[:, which : which + 1] * got_row
        gate_grads.append(jnp.sum(dy_wide * got_row, axis=1))
        row_sum = row_sum + back_rows[which]
    layer_output = mixed.astype(jnp.bfloat16)
    gate_grad = jnp.stack(gate_grads, axis=1)
    cross_term = jnp.sum(gate_grad * gate_value, axis=1, keepdims=True)
    pick_delta = (gate_grad - cross_term) / pick_sum * picked * (1.0 - picked)
    logit_grad = jnp.sum(picker * pick_delta[:, :, None], axis=1)
    grad_tokens = (row_sum + jnp.dot(logit_grad, w_router.T, precision=highest)).astype(
        jnp.bfloat16
    )
    router_part = jnp.dot(tokens_wide.T, logit_grad, precision=highest)
    grad_router = all_sum(all_sum(router_part, "dp"), "expert")
    return (layer_output, grad_tokens, grad_router, grad_gate, grad_up, grad_down)


def solution(mesh):
    return jax.shard_map(
        on_device,
        mesh=mesh,
        in_specs=(
            P(("dp", "expert"), None),
            P(("dp", "expert"), None),
            P(("dp", "expert"), None),
            P(),
            P("expert", None, None),
            P("expert", None, None),
            P("expert", None, None),
            P(("dp", "expert"), None),
        ),
        out_specs=(
            P(("dp", "expert"), None),
            P(("dp", "expert"), None),
            P(),
            P("expert", "dp", None),
            P("expert", "dp", None),
            P("expert", "dp", None),
        ),
        check_vma=False,
    )
```

```python
import jax
import jax.numpy as jnp
from jax import lax
from jax.sharding import PartitionSpec as P
from jax.experimental import pallas as pl


def silu_parts(hidden):
    sigmoid_val = jax.nn.sigmoid(hidden)
    return (hidden * sigmoid_val, sigmoid_val * (1.0 + hidden * (1.0 - sigmoid_val)))


def group_sum(value, axis, low_bit, bits):
    size = lax.axis_size(axis)
    got = [value]
    for offset in range(1, 2**bits):
        step = offset << low_bit
        pairs = [(i, i ^ step) for i in range(size)]
        got.append(lax.ppermute(value, axis, pairs))
    while len(got) > 1:
        got = [got[i] + got[i + 1] for i in range(0, len(got), 2)]
    return got[0]


def all_sum(value, axis):
    size = lax.axis_size(axis)
    low_bit = 0
    while (1 << low_bit) < size:
        bits = min(3, (size - 1).bit_length() - low_bit)
        value = group_sum(value, axis, low_bit, bits)
        low_bit += bits
    return value


def weight_grad_kernel(rows_ref, grads_ref, deltas_ref, act_ref, out_ref):
    split = deltas_ref.shape[1]
    inner = (((0,), (0,)), ((), ()))
    both = lax.dot_general(rows_ref[...], deltas_ref[...], inner, preferred_element_type=jnp.float32)
    down = lax.dot_general(grads_ref[...], act_ref[...], inner, preferred_element_type=jnp.float32)
    out_ref[:, :split] = both.astype(out_ref.dtype)
    out_ref[:, split:] = down.astype(out_ref.dtype)


def weight_grads(rows, grads, gate_delta, up_delta, activated):
    width = rows.shape[1]
    count = rows.shape[0]
    hidden = activated.shape[1]
    deltas = jnp.concatenate([gate_delta, up_delta], axis=1)
    tile = 512
    return pl.pallas_call(
        weight_grad_kernel,
        grid=(width // tile,),
        in_specs=[
            pl.BlockSpec((count, tile), lambda i: (0, i)),
            pl.BlockSpec((count, tile), lambda i: (0, i)),
            pl.BlockSpec((count, 2 * hidden), lambda i: (0, 0)),
            pl.BlockSpec((count, hidden), lambda i: (0, 0)),
        ],
        out_specs=pl.BlockSpec((tile, 3 * hidden), lambda i: (i, 0)),
        out_shape=jax.ShapeDtypeStruct((width, 3 * hidden), jnp.bfloat16),
    )(rows, grads, deltas, activated)


def halving_scatter(parts, axis):
    size = lax.axis_size(axis)
    me = lax.axis_index(axis)
    rows = parts.shape[0] // size
    acc = parts.reshape(size, rows, parts.shape[1]).astype(jnp.float32)
    bits = (size - 1).bit_length()
    for bit in range(bits):
        cur = acc.reshape(size >> (bit + 1), 2, rows, parts.shape[1])
        mine = (me >> bit) & 1
        keep = lax.dynamic_index_in_dim(cur, mine, axis=1, keepdims=False)
        send = lax.dynamic_index_in_dim(cur, 1 - mine, axis=1, keepdims=False)
        if bit < 3:
            send = send.astype(jnp.bfloat16)
        pairs = [(i, i ^ (1 << bit)) for i in range(size)]
        acc = keep + lax.ppermute(send, axis, pairs).astype(jnp.float32)
    return acc.reshape(rows, parts.shape[1])


def on_device(tokens, expert_ids, slot_index, w_router, w_gate, w_up, w_down, grad_out):
    tok_count, width = tokens.shape
    choice_count = expert_ids.shape[1]
    expert_count = w_router.shape[1]
    local_count = w_gate.shape[0]
    hidden_width = w_gate.shape[2]
    sender_count = lax.axis_size("expert")
    own_rows = width // lax.axis_size("dp")
    slot_count = tok_count * choice_count // expert_count
    highest = lax.Precision.HIGHEST
    tokens_wide = tokens.astype(jnp.float32)
    scores = jax.nn.sigmoid(jnp.dot(tokens_wide, w_router, precision=highest))
    picker = (
        expert_ids[:, :, None] == jnp.arange(expert_count, dtype=jnp.int32)[None, None, :]
    ).astype(jnp.float32)
    picked = jnp.sum(picker * scores[:, None, :], axis=2)
    pick_sum = jnp.sum(picked, axis=1, keepdims=True)
    gate_value = picked / pick_sum
    is_live = slot_index >= 0
    live_gate = jnp.where(is_live, gate_value, 0.0)
    position = jnp.where(is_live, expert_ids * slot_count + slot_index, expert_count * slot_count)
    slot_total = expert_count * slot_count
    chosen = position[:, :, None] == jnp.arange(slot_total, dtype=jnp.int32)[None, None, :]
    slot_of_token = jnp.any(chosen, axis=1)
    gate_of_slot = jnp.sum(jnp.where(chosen, live_gate[:, :, None], 0.0), axis=(0, 1))
    pick_rows = slot_of_token.astype(jnp.bfloat16)
    outgoing = jnp.dot(pick_rows.T, tokens, preferred_element_type=jnp.float32).astype(jnp.bfloat16)
    picked_grad = jnp.dot(pick_rows.T, grad_out, preferred_element_type=jnp.float32)
    grad_rows = (gate_of_slot[:, None] * picked_grad).astype(jnp.bfloat16)
    outgoing = outgoing.reshape(expert_count, slot_count, width)
    grad_rows = grad_rows.reshape(expert_count, slot_count, width)
    both_in = lax.all_to_all(
        jnp.concatenate([outgoing, grad_rows], axis=1), "expert", split_axis=0, concat_axis=0, tiled=True
    )
    block_shape = (sender_count, local_count, slot_count, width)
    row_block = both_in[:, :slot_count].reshape(block_shape)
    arrived = both_in[:, slot_count:].reshape(block_shape)
    hidden_gate = jnp.einsum(
        "slnd,ldf->slnf", row_block, w_gate, preferred_element_type=jnp.float32
    )
    hidden_up = jnp.einsum(
        "slnd,ldf->slnf", row_block, w_up, preferred_element_type=jnp.float32
    )
    silu_value, silu_slope = silu_parts(hidden_gate)
    activated = (silu_value * hidden_up).astype(jnp.bfloat16)
    expert_out = jnp.einsum(
        "slnf,ldf->slnd", activated, w_down, preferred_element_type=jnp.float32
    ).astype(jnp.bfloat16)
    flat_rows = (sender_count * local_count, slot_count, width)
    returned = lax.all_to_all(
        expert_out.reshape(flat_rows), "expert", split_axis=0, concat_axis=0, tiled=True
    )
    grad_act = jnp.einsum("slnd,ldf->slnf", arrived, w_down, preferred_element_type=jnp.float32)
    gate_delta = (grad_act * hidden_up * silu_slope).astype(jnp.bfloat16)
    up_delta = (grad_act * silu_value).astype(jnp.bfloat16)
    row_grad = (
        jnp.einsum("slnf,ldf->slnd", gate_delta, w_gate, preferred_element_type=jnp.float32)
        + jnp.einsum("slnf,ldf->slnd", up_delta, w_up, preferred_element_type=jnp.float32)
    ).astype(jnp.bfloat16)
    sent_back = lax.all_to_all(
        row_grad.reshape(flat_rows), "expert", split_axis=0, concat_axis=0, tiled=True
    )
    if local_count == 1:
        flat = (sender_count * slot_count, -1)
        partials = weight_grads(
            row_block.reshape(flat),
            arrived.reshape(flat),
            gate_delta.reshape(flat),
            up_delta.reshape(flat),
            activated.reshape(flat),
        )
    else:
        gate_part = jnp.einsum("slnd,slnf->dlf", row_block, gate_delta, preferred_element_type=jnp.float32)
        up_part = jnp.einsum("slnd,slnf->dlf", row_block, up_delta, preferred_element_type=jnp.float32)
        down_part = jnp.einsum("slnd,slnf->dlf", arrived, activated, preferred_element_type=jnp.float32)
        partials = (
            jnp.concatenate([gate_part, up_part, down_part], axis=2)
            .reshape(lax.axis_size("dp") * own_rows, local_count * 3 * hidden_width)
            .astype(jnp.bfloat16)
        )
    joined = halving_scatter(partials, "dp")
    triple_view = joined.reshape(-1, local_count, 3, hidden_width)
    grad_gate = jnp.transpose(triple_view[:, :, 0, :], (1, 0, 2))
    grad_up = jnp.transpose(triple_view[:, :, 1, :], (1, 0, 2))
    grad_down = jnp.transpose(triple_view[:, :, 2, :], (1, 0, 2))
    choice_rows = jnp.transpose(chosen, (1, 0, 2)).reshape(choice_count * tok_count, slot_total)
    choice_rows = choice_rows.astype(jnp.bfloat16)
    got_rows = jnp.dot(
        choice_rows, returned.reshape(slot_total, width), preferred_element_type=jnp.float32
    ).reshape(choice_count, tok_count, width)
    back_rows = jnp.dot(
        choice_rows, sent_back.reshape(slot_total, width), preferred_element_type=jnp.float32
    ).reshape(choice_count, tok_count, width)
    dy_wide = grad_out.astype(jnp.float32)
    mixed = jnp.zeros((tok_count, width), jnp.float32)
    row_sum = jnp.zeros((tok_count, width), jnp.float32)
    gate_grads = []
    for which in range(choice_count):
        got_row = got_rows[which]
        mixed = mixed + live_gate[:, which : which + 1] * got_row
        gate_grads.append(jnp.sum(dy_wide * got_row, axis=1))
        row_sum = row_sum + back_rows[which]
    layer_output = mixed.astype(jnp.bfloat16)
    gate_grad = jnp.stack(gate_grads, axis=1)
    cross_term = jnp.sum(gate_grad * gate_value, axis=1, keepdims=True)
    pick_delta = (gate_grad - cross_term) / pick_sum * picked * (1.0 - picked)
    logit_grad = jnp.sum(picker * pick_delta[:, :, None], axis=1)
    grad_tokens = (row_sum + jnp.dot(logit_grad, w_router.T, precision=highest)).astype(
        jnp.bfloat16
    )
    router_part = jnp.dot(tokens_wide.T, logit_grad, precision=highest)
    grad_router = all_sum(all_sum(router_part, "dp"), "expert")
    return (layer_output, grad_tokens, grad_router, grad_gate, grad_up, grad_down)


def solution(mesh):
    return jax.shard_map(
        on_device,
        mesh=mesh,
        in_specs=(
            P(("dp", "expert"), None),
            P(("dp", "expert"), None),
            P(("dp", "expert"), None),
            P(),
            P("expert", None, None),
            P("expert", None, None),
            P("expert", None, None),
            P(("dp", "expert"), None),
        ),
        out_specs=(
            P(("dp", "expert"), None),
            P(("dp", "expert"), None),
            P(),
            P("expert", "dp", None),
            P("expert", "dp", None),
            P("expert", "dp", None),
        ),
        check_vma=False,
    )
```

```python
import jax
import jax.numpy as jnp
from jax import lax
from jax.sharding import PartitionSpec as P
from jax.experimental import pallas as pl


def silu_parts(hidden):
    sigmoid_val = jax.nn.sigmoid(hidden)
    return (hidden * sigmoid_val, sigmoid_val * (1.0 + hidden * (1.0 - sigmoid_val)))


def group_sum(value, axis, low_bit, bits):
    size = lax.axis_size(axis)
    got = [value]
    for offset in range(1, 2**bits):
        step = offset << low_bit
        pairs = [(i, i ^ step) for i in range(size)]
        got.append(lax.ppermute(value, axis, pairs))
    while len(got) > 1:
        got = [got[i] + got[i + 1] for i in range(0, len(got), 2)]
    return got[0]


def all_sum(value, axis):
    size = lax.axis_size(axis)
    low_bit = 0
    while (1 << low_bit) < size:
        bits = min(3, (size - 1).bit_length() - low_bit)
        value = group_sum(value, axis, low_bit, bits)
        low_bit += bits
    return value


def weight_grad_kernel(rows_ref, grads_ref, gate_ref, up_ref, act_ref, out_ref):
    split = gate_ref.shape[1]
    inner = (((0,), (0,)), ((), ()))
    rows = rows_ref[...]
    for col, (lhs, rhs) in enumerate(((rows, gate_ref), (rows, up_ref), (grads_ref[...], act_ref))):
        part = lax.dot_general(lhs, rhs[...], inner, preferred_element_type=jnp.float32)
        out_ref[:, col * split : (col + 1) * split] = part.astype(out_ref.dtype)


def weight_grads(rows, grads, gate_delta, up_delta, activated):
    width = rows.shape[1]
    count = rows.shape[0]
    hidden = activated.shape[1]
    tile = 1024
    return pl.pallas_call(
        weight_grad_kernel,
        grid=(width // tile,),
        in_specs=[
            pl.BlockSpec((count, tile), lambda i: (0, i)),
            pl.BlockSpec((count, tile), lambda i: (0, i)),
            pl.BlockSpec((count, hidden), lambda i: (0, 0)),
            pl.BlockSpec((count, hidden), lambda i: (0, 0)),
            pl.BlockSpec((count, hidden), lambda i: (0, 0)),
        ],
        out_specs=pl.BlockSpec((tile, 3 * hidden), lambda i: (i, 0)),
        out_shape=jax.ShapeDtypeStruct((width, 3 * hidden), jnp.bfloat16),
    )(rows, grads, gate_delta, up_delta, activated)


def on_device(tokens, expert_ids, slot_index, w_router, w_gate, w_up, w_down, grad_out):
    tok_count, width = tokens.shape
    choice_count = expert_ids.shape[1]
    expert_count = w_router.shape[1]
    local_count = w_gate.shape[0]
    hidden_width = w_gate.shape[2]
    sender_count = lax.axis_size("expert")
    own_rows = width // lax.axis_size("dp")
    slot_count = tok_count * choice_count // expert_count
    highest = lax.Precision.HIGHEST
    tokens_wide = tokens.astype(jnp.float32)
    scores = jax.nn.sigmoid(jnp.dot(tokens_wide, w_router, precision=highest))
    picker = (
        expert_ids[:, :, None] == jnp.arange(expert_count, dtype=jnp.int32)[None, None, :]
    ).astype(jnp.float32)
    picked = jnp.sum(picker * scores[:, None, :], axis=2)
    pick_sum = jnp.sum(picked, axis=1, keepdims=True)
    gate_value = picked / pick_sum
    is_live = slot_index >= 0
    live_gate = jnp.where(is_live, gate_value, 0.0)
    position = jnp.where(is_live, expert_ids * slot_count + slot_index, expert_count * slot_count)
    slot_total = expert_count * slot_count
    chosen = position[:, :, None] == jnp.arange(slot_total, dtype=jnp.int32)[None, None, :]
    slot_of_token = jnp.any(chosen, axis=1)
    gate_of_slot = jnp.sum(jnp.where(chosen, live_gate[:, :, None], 0.0), axis=(0, 1))
    pick_rows = slot_of_token.astype(jnp.bfloat16)
    outgoing = jnp.dot(pick_rows.T, tokens, preferred_element_type=jnp.float32).astype(jnp.bfloat16)
    picked_grad = jnp.dot(pick_rows.T, grad_out, preferred_element_type=jnp.float32)
    grad_rows = (gate_of_slot[:, None] * picked_grad).astype(jnp.bfloat16)
    outgoing = outgoing.reshape(expert_count, slot_count, width)
    grad_rows = grad_rows.reshape(expert_count, slot_count, width)
    both_in = lax.all_to_all(
        jnp.concatenate([outgoing, grad_rows], axis=1), "expert", split_axis=0, concat_axis=0, tiled=True
    )
    block_shape = (sender_count, local_count, slot_count, width)
    row_block = both_in[:, :slot_count].reshape(block_shape)
    arrived = both_in[:, slot_count:].reshape(block_shape)
    hidden_gate = jnp.einsum(
        "slnd,ldf->slnf", row_block, w_gate, preferred_element_type=jnp.float32
    )
    hidden_up = jnp.einsum(
        "slnd,ldf->slnf", row_block, w_up, preferred_element_type=jnp.float32
    )
    silu_value, silu_slope = silu_parts(hidden_gate)
    activated = (silu_value * hidden_up).astype(jnp.bfloat16)
    expert_out = jnp.einsum(
        "slnf,ldf->slnd", activated, w_down, preferred_element_type=jnp.float32
    ).astype(jnp.bfloat16)
    flat_rows = (sender_count * local_count, slot_count, width)
    returned = lax.all_to_all(
        expert_out.reshape(flat_rows), "expert", split_axis=0, concat_axis=0, tiled=True
    )
    grad_act = jnp.einsum("slnd,ldf->slnf", arrived, w_down, preferred_element_type=jnp.float32)
    gate_delta = (grad_act * hidden_up * silu_slope).astype(jnp.bfloat16)
    up_delta = (grad_act * silu_value).astype(jnp.bfloat16)
    row_grad = (
        jnp.einsum("slnf,ldf->slnd", gate_delta, w_gate, preferred_element_type=jnp.float32)
        + jnp.einsum("slnf,ldf->slnd", up_delta, w_up, preferred_element_type=jnp.float32)
    ).astype(jnp.bfloat16)
    sent_back = lax.all_to_all(
        row_grad.reshape(flat_rows), "expert", split_axis=0, concat_axis=0, tiled=True
    )
    if local_count == 1:
        flat = (sender_count * slot_count, -1)
        partials = weight_grads(
            row_block.reshape(flat),
            arrived.reshape(flat),
            gate_delta.reshape(flat),
            up_delta.reshape(flat),
            activated.reshape(flat),
        )
    else:
        gate_part = jnp.einsum("slnd,slnf->dlf", row_block, gate_delta, preferred_element_type=jnp.float32)
        up_part = jnp.einsum("slnd,slnf->dlf", row_block, up_delta, preferred_element_type=jnp.float32)
        down_part = jnp.einsum("slnd,slnf->dlf", arrived, activated, preferred_element_type=jnp.float32)
        partials = (
            jnp.concatenate([gate_part, up_part, down_part], axis=2)
            .reshape(lax.axis_size("dp") * own_rows, local_count * 3 * hidden_width)
            .astype(jnp.bfloat16)
        )
    joined = lax.psum_scatter(partials, "dp", scatter_dimension=0, tiled=True).astype(jnp.float32)
    triple_view = joined.reshape(-1, local_count, 3, hidden_width)
    grad_gate = jnp.transpose(triple_view[:, :, 0, :], (1, 0, 2))
    grad_up = jnp.transpose(triple_view[:, :, 1, :], (1, 0, 2))
    grad_down = jnp.transpose(triple_view[:, :, 2, :], (1, 0, 2))
    choice_rows = jnp.transpose(chosen, (1, 0, 2)).reshape(choice_count * tok_count, slot_total)
    choice_rows = choice_rows.astype(jnp.bfloat16)
    got_rows = jnp.dot(
        choice_rows, returned.reshape(slot_total, width), preferred_element_type=jnp.float32
    ).reshape(choice_count, tok_count, width)
    back_rows = jnp.dot(
        choice_rows, sent_back.reshape(slot_total, width), preferred_element_type=jnp.float32
    ).reshape(choice_count, tok_count, width)
    dy_wide = grad_out.astype(jnp.float32)
    mixed = jnp.zeros((tok_count, width), jnp.float32)
    row_sum = jnp.zeros((tok_count, width), jnp.float32)
    gate_grads = []
    for which in range(choice_count):
        got_row = got_rows[which]
        mixed = mixed + live_gate[:, which : which + 1] * got_row
        gate_grads.append(jnp.sum(dy_wide * got_row, axis=1))
        row_sum = row_sum + back_rows[which]
    layer_output = mixed.astype(jnp.bfloat16)
    gate_grad = jnp.stack(gate_grads, axis=1)
    cross_term = jnp.sum(gate_grad * gate_value, axis=1, keepdims=True)
    pick_delta = (gate_grad - cross_term) / pick_sum * picked * (1.0 - picked)
    logit_grad = jnp.sum(picker * pick_delta[:, :, None], axis=1)
    grad_tokens = (row_sum + jnp.dot(logit_grad, w_router.T, precision=highest)).astype(
        jnp.bfloat16
    )
    router_part = jnp.dot(tokens_wide.T, logit_grad, precision=highest)
    grad_router = all_sum(all_sum(router_part, "dp"), "expert")
    return (layer_output, grad_tokens, grad_router, grad_gate, grad_up, grad_down)


def solution(mesh):
    return jax.shard_map(
        on_device,
        mesh=mesh,
        in_specs=(
            P(("dp", "expert"), None),
            P(("dp", "expert"), None),
            P(("dp", "expert"), None),
            P(),
            P("expert", None, None),
            P("expert", None, None),
            P("expert", None, None),
            P(("dp", "expert"), None),
        ),
        out_specs=(
            P(("dp", "expert"), None),
            P(("dp", "expert"), None),
            P(),
            P("expert", "dp", None),
            P("expert", "dp", None),
            P("expert", "dp", None),
        ),
        check_vma=False,
    )
```

```python
import jax
import jax.numpy as jnp
from jax import lax
from jax.sharding import PartitionSpec as P
from jax.experimental import pallas as pl


def silu_parts(hidden):
    sigmoid_val = jax.nn.sigmoid(hidden)
    return (hidden * sigmoid_val, sigmoid_val * (1.0 + hidden * (1.0 - sigmoid_val)))


def group_sum(value, axis, low_bit, bits):
    size = lax.axis_size(axis)
    got = [value]
    for offset in range(1, 2**bits):
        step = offset << low_bit
        pairs = [(i, i ^ step) for i in range(size)]
        got.append(lax.ppermute(value, axis, pairs))
    while len(got) > 1:
        got = [got[i] + got[i + 1] for i in range(0, len(got), 2)]
    return got[0]


def all_sum(value, axis):
    size = lax.axis_size(axis)
    low_bit = 0
    while (1 << low_bit) < size:
        bits = min(3, (size - 1).bit_length() - low_bit)
        value = group_sum(value, axis, low_bit, bits)
        low_bit += bits
    return value


def weight_grad_kernel(rows_ref, grads_ref, deltas_ref, act_ref, out_ref):
    split = deltas_ref.shape[1]
    inner = (((0,), (0,)), ((), ()))
    both = lax.dot_general(rows_ref[...], deltas_ref[...], inner, preferred_element_type=jnp.float32)
    down = lax.dot_general(grads_ref[...], act_ref[...], inner, preferred_element_type=jnp.float32)
    out_ref[:, :split] = both.astype(out_ref.dtype)
    out_ref[:, split:] = down.astype(out_ref.dtype)


def weight_grads(rows, grads, gate_delta, up_delta, activated):
    width = rows.shape[1]
    count = rows.shape[0]
    hidden = activated.shape[1]
    deltas = jnp.concatenate([gate_delta, up_delta], axis=1)
    tile = 512
    return pl.pallas_call(
        weight_grad_kernel,
        grid=(width // tile,),
        in_specs=[
            pl.BlockSpec((count, tile), lambda i: (0, i)),
            pl.BlockSpec((count, tile), lambda i: (0, i)),
            pl.BlockSpec((count, 2 * hidden), lambda i: (0, 0)),
            pl.BlockSpec((count, hidden), lambda i: (0, 0)),
        ],
        out_specs=pl.BlockSpec((tile, 3 * hidden), lambda i: (i, 0)),
        out_shape=jax.ShapeDtypeStruct((width, 3 * hidden), jnp.bfloat16),
    )(rows, grads, deltas, activated)


def on_device(tokens, expert_ids, slot_index, w_router, w_gate, w_up, w_down, grad_out):
    tok_count, width = tokens.shape
    choice_count = expert_ids.shape[1]
    expert_count = w_router.shape[1]
    local_count = w_gate.shape[0]
    hidden_width = w_gate.shape[2]
    sender_count = lax.axis_size("expert")
    own_rows = width // lax.axis_size("dp")
    slot_count = tok_count * choice_count // expert_count
    highest = lax.Precision.HIGHEST
    tokens_wide = tokens.astype(jnp.float32)
    scores = jax.nn.sigmoid(jnp.dot(tokens_wide, w_router, precision=highest))
    picker = (
        expert_ids[:, :, None] == jnp.arange(expert_count, dtype=jnp.int32)[None, None, :]
    ).astype(jnp.float32)
    picked = jnp.sum(picker * scores[:, None, :], axis=2)
    pick_sum = jnp.sum(picked, axis=1, keepdims=True)
    gate_value = picked / pick_sum
    is_live = slot_index >= 0
    live_gate = jnp.where(is_live, gate_value, 0.0)
    position = jnp.where(is_live, expert_ids * slot_count + slot_index, expert_count * slot_count)
    slot_total = expert_count * slot_count
    chosen = position[:, :, None] == jnp.arange(slot_total, dtype=jnp.int32)[None, None, :]
    slot_of_token = jnp.any(chosen, axis=1)
    gate_of_slot = jnp.sum(jnp.where(chosen, live_gate[:, :, None], 0.0), axis=(0, 1))
    pick_rows = slot_of_token.astype(jnp.bfloat16)
    outgoing = jnp.dot(pick_rows.T, tokens, preferred_element_type=jnp.float32).astype(jnp.bfloat16)
    picked_grad = jnp.dot(pick_rows.T, grad_out, preferred_element_type=jnp.float32)
    grad_rows = (gate_of_slot[:, None] * picked_grad).astype(jnp.bfloat16)
    outgoing = outgoing.reshape(expert_count, slot_count, width)
    grad_rows = grad_rows.reshape(expert_count, slot_count, width)
    block_shape = (sender_count, local_count, slot_count, width)
    row_block = lax.all_to_all(outgoing, "expert", split_axis=0, concat_axis=0, tiled=True).reshape(block_shape)
    arrived = lax.all_to_all(grad_rows, "expert", split_axis=0, concat_axis=0, tiled=True).reshape(block_shape)
    hidden_gate = jnp.einsum(
        "slnd,ldf->slnf", row_block, w_gate, preferred_element_type=jnp.float32
    )
    hidden_up = jnp.einsum(
        "slnd,ldf->slnf", row_block, w_up, preferred_element_type=jnp.float32
    )
    silu_value, silu_slope = silu_parts(hidden_gate)
    activated = (silu_value * hidden_up).astype(jnp.bfloat16)
    expert_out = jnp.einsum(
        "slnf,ldf->slnd", activated, w_down, preferred_element_type=jnp.float32
    ).astype(jnp.bfloat16)
    flat_rows = (sender_count * local_count, slot_count, width)
    returned = lax.all_to_all(
        expert_out.reshape(flat_rows), "expert", split_axis=0, concat_axis=0, tiled=True
    )
    grad_act = jnp.einsum("slnd,ldf->slnf", arrived, w_down, preferred_element_type=jnp.float32)
    gate_delta = (grad_act * hidden_up * silu_slope).astype(jnp.bfloat16)
    up_delta = (grad_act * silu_value).astype(jnp.bfloat16)
    row_grad = (
        jnp.einsum("slnf,ldf->slnd", gate_delta, w_gate, preferred_element_type=jnp.float32)
        + jnp.einsum("slnf,ldf->slnd", up_delta, w_up, preferred_element_type=jnp.float32)
    ).astype(jnp.bfloat16)
    sent_back = lax.all_to_all(
        row_grad.reshape(flat_rows), "expert", split_axis=0, concat_axis=0, tiled=True
    )
    if local_count == 1:
        flat = (sender_count * slot_count, -1)
        partials = weight_grads(
            row_block.reshape(flat),
            arrived.reshape(flat),
            gate_delta.reshape(flat),
            up_delta.reshape(flat),
            activated.reshape(flat),
        )
    else:
        gate_part = jnp.einsum("slnd,slnf->dlf", row_block, gate_delta, preferred_element_type=jnp.float32)
        up_part = jnp.einsum("slnd,slnf->dlf", row_block, up_delta, preferred_element_type=jnp.float32)
        down_part = jnp.einsum("slnd,slnf->dlf", arrived, activated, preferred_element_type=jnp.float32)
        partials = (
            jnp.concatenate([gate_part, up_part, down_part], axis=2)
            .reshape(lax.axis_size("dp") * own_rows, local_count * 3 * hidden_width)
            .astype(jnp.bfloat16)
        )
    joined = lax.psum_scatter(partials, "dp", scatter_dimension=0, tiled=True).astype(jnp.float32)
    triple_view = joined.reshape(-1, local_count, 3, hidden_width)
    grad_gate = jnp.transpose(triple_view[:, :, 0, :], (1, 0, 2))
    grad_up = jnp.transpose(triple_view[:, :, 1, :], (1, 0, 2))
    grad_down = jnp.transpose(triple_view[:, :, 2, :], (1, 0, 2))
    choice_rows = jnp.transpose(chosen, (1, 0, 2)).reshape(choice_count * tok_count, slot_total)
    choice_rows = choice_rows.astype(jnp.bfloat16)
    got_rows = jnp.dot(
        choice_rows, returned.reshape(slot_total, width), preferred_element_type=jnp.float32
    ).reshape(choice_count, tok_count, width)
    back_rows = jnp.dot(
        choice_rows, sent_back.reshape(slot_total, width), preferred_element_type=jnp.float32
    ).reshape(choice_count, tok_count, width)
    dy_wide = grad_out.astype(jnp.float32)
    mixed = jnp.zeros((tok_count, width), jnp.float32)
    row_sum = jnp.zeros((tok_count, width), jnp.float32)
    gate_grads = []
    for which in range(choice_count):
        got_row = got_rows[which]
        mixed = mixed + live_gate[:, which : which + 1] * got_row
        gate_grads.append(jnp.sum(dy_wide * got_row, axis=1))
        row_sum = row_sum + back_rows[which]
    layer_output = mixed.astype(jnp.bfloat16)
    gate_grad = jnp.stack(gate_grads, axis=1)
    cross_term = jnp.sum(gate_grad * gate_value, axis=1, keepdims=True)
    pick_delta = (gate_grad - cross_term) / pick_sum * picked * (1.0 - picked)
    logit_grad = jnp.sum(picker * pick_delta[:, :, None], axis=1)
    grad_tokens = (row_sum + jnp.dot(logit_grad, w_router.T, precision=highest)).astype(
        jnp.bfloat16
    )
    router_part = jnp.dot(tokens_wide.T, logit_grad, precision=highest)
    grad_router = all_sum(all_sum(router_part, "dp"), "expert")
    return (layer_output, grad_tokens, grad_router, grad_gate, grad_up, grad_down)


def solution(mesh):
    return jax.shard_map(
        on_device,
        mesh=mesh,
        in_specs=(
            P(("dp", "expert"), None),
            P(("dp", "expert"), None),
            P(("dp", "expert"), None),
            P(),
            P("expert", None, None),
            P("expert", None, None),
            P("expert", None, None),
            P(("dp", "expert"), None),
        ),
        out_specs=(
            P(("dp", "expert"), None),
            P(("dp", "expert"), None),
            P(),
            P("expert", "dp", None),
            P("expert", "dp", None),
            P("expert", "dp", None),
        ),
        check_vma=False,
    )
```

```python
import jax
import jax.numpy as jnp
from jax import lax
from jax.sharding import PartitionSpec as P
from jax.experimental import pallas as pl


def silu_parts(hidden):
    sigmoid_val = jax.nn.sigmoid(hidden)
    return (hidden * sigmoid_val, sigmoid_val * (1.0 + hidden * (1.0 - sigmoid_val)))


def group_sum(value, axis, low_bit, bits):
    size = lax.axis_size(axis)
    got = [value]
    for offset in range(1, 2**bits):
        step = offset << low_bit
        pairs = [(i, i ^ step) for i in range(size)]
        got.append(lax.ppermute(value, axis, pairs))
    while len(got) > 1:
        got = [got[i] + got[i + 1] for i in range(0, len(got), 2)]
    return got[0]


def all_sum(value, axis):
    size = lax.axis_size(axis)
    low_bit = 0
    while (1 << low_bit) < size:
        bits = min(3, (size - 1).bit_length() - low_bit)
        value = group_sum(value, axis, low_bit, bits)
        low_bit += bits
    return value


def weight_grad_kernel(rows_ref, grads_ref, deltas_ref, act_ref, out_ref):
    split = deltas_ref.shape[1]
    inner = (((0,), (0,)), ((), ()))
    both = lax.dot_general(rows_ref[...], deltas_ref[...], inner, preferred_element_type=jnp.float32)
    down = lax.dot_general(grads_ref[...], act_ref[...], inner, preferred_element_type=jnp.float32)
    out_ref[:, :split] = both.astype(out_ref.dtype)
    out_ref[:, split:] = down.astype(out_ref.dtype)


def weight_grads(rows, grads, gate_delta, up_delta, activated):
    width = rows.shape[1]
    count = rows.shape[0]
    hidden = activated.shape[1]
    deltas = jnp.concatenate([gate_delta, up_delta], axis=1)
    tile = 512
    return pl.pallas_call(
        weight_grad_kernel,
        grid=(width // tile,),
        in_specs=[
            pl.BlockSpec((count, tile), lambda i: (0, i)),
            pl.BlockSpec((count, tile), lambda i: (0, i)),
            pl.BlockSpec((count, 2 * hidden), lambda i: (0, 0)),
            pl.BlockSpec((count, hidden), lambda i: (0, 0)),
        ],
        out_specs=pl.BlockSpec((tile, 3 * hidden), lambda i: (i, 0)),
        out_shape=jax.ShapeDtypeStruct((width, 3 * hidden), jnp.bfloat16),
    )(rows, grads, deltas, activated)


def on_device(tokens, expert_ids, slot_index, w_router, w_gate, w_up, w_down, grad_out):
    tok_count, width = tokens.shape
    choice_count = expert_ids.shape[1]
    expert_count = w_router.shape[1]
    local_count = w_gate.shape[0]
    hidden_width = w_gate.shape[2]
    sender_count = lax.axis_size("expert")
    own_rows = width // lax.axis_size("dp")
    slot_count = tok_count * choice_count // expert_count
    highest = lax.Precision.HIGHEST
    tokens_wide = tokens.astype(jnp.float32)
    scores = jax.nn.sigmoid(jnp.dot(tokens_wide, w_router, precision=highest))
    picker = (
        expert_ids[:, :, None] == jnp.arange(expert_count, dtype=jnp.int32)[None, None, :]
    ).astype(jnp.float32)
    picked = jnp.sum(picker * scores[:, None, :], axis=2)
    pick_sum = jnp.sum(picked, axis=1, keepdims=True)
    gate_value = picked / pick_sum
    is_live = slot_index >= 0
    live_gate = jnp.where(is_live, gate_value, 0.0)
    position = jnp.where(is_live, expert_ids * slot_count + slot_index, expert_count * slot_count)
    slot_total = expert_count * slot_count
    chosen = position[:, :, None] == jnp.arange(slot_total, dtype=jnp.int32)[None, None, :]
    slot_of_token = jnp.any(chosen, axis=1)
    gate_of_slot = jnp.sum(jnp.where(chosen, live_gate[:, :, None], 0.0), axis=(0, 1))
    pick_rows = slot_of_token.astype(jnp.bfloat16)
    outgoing = jnp.dot(pick_rows.T, tokens, preferred_element_type=jnp.float32).astype(jnp.bfloat16)
    picked_grad = jnp.dot(pick_rows.T, grad_out, preferred_element_type=jnp.float32)
    grad_rows = (gate_of_slot[:, None] * picked_grad).astype(jnp.bfloat16)
    outgoing = outgoing.reshape(expert_count, slot_count, width)
    grad_rows = grad_rows.reshape(expert_count, slot_count, width)
    both_in = lax.all_to_all(
        jnp.concatenate([outgoing, grad_rows], axis=1), "expert", split_axis=0, concat_axis=0, tiled=True
    )
    block_shape = (sender_count, local_count, slot_count, width)
    row_block = both_in[:, :slot_count].reshape(block_shape)
    arrived = both_in[:, slot_count:].reshape(block_shape)
    hidden_gate = jnp.einsum(
        "slnd,ldf->slnf", row_block, w_gate, preferred_element_type=jnp.float32
    )
    hidden_up = jnp.einsum(
        "slnd,ldf->slnf", row_block, w_up, preferred_element_type=jnp.float32
    )
    silu_value, silu_slope = silu_parts(hidden_gate)
    activated = (silu_value * hidden_up).astype(jnp.bfloat16)
    expert_out = jnp.einsum(
        "slnf,ldf->slnd", activated, w_down, preferred_element_type=jnp.float32
    ).astype(jnp.bfloat16)
    flat_rows = (sender_count * local_count, slot_count, width)
    returned = lax.all_to_all(
        expert_out.reshape(flat_rows), "expert", split_axis=0, concat_axis=0, tiled=True
    )
    grad_act = jnp.einsum("slnd,ldf->slnf", arrived, w_down, preferred_element_type=jnp.float32)
    gate_delta = (grad_act * hidden_up * silu_slope).astype(jnp.bfloat16)
    up_delta = (grad_act * silu_value).astype(jnp.bfloat16)
    row_grad = (
        jnp.einsum("slnf,ldf->slnd", gate_delta, w_gate, preferred_element_type=jnp.float32)
        + jnp.einsum("slnf,ldf->slnd", up_delta, w_up, preferred_element_type=jnp.float32)
    ).astype(jnp.bfloat16)
    sent_back = lax.all_to_all(
        row_grad.reshape(flat_rows), "expert", split_axis=0, concat_axis=0, tiled=True
    )
    if local_count == 1:
        flat = (sender_count * slot_count, -1)
        partials = weight_grads(
            row_block.reshape(flat),
            arrived.reshape(flat),
            gate_delta.reshape(flat),
            up_delta.reshape(flat),
            activated.reshape(flat),
        )
    else:
        gate_part = jnp.einsum("slnd,slnf->dlf", row_block, gate_delta, preferred_element_type=jnp.float32)
        up_part = jnp.einsum("slnd,slnf->dlf", row_block, up_delta, preferred_element_type=jnp.float32)
        down_part = jnp.einsum("slnd,slnf->dlf", arrived, activated, preferred_element_type=jnp.float32)
        partials = (
            jnp.concatenate([gate_part, up_part, down_part], axis=2)
            .reshape(lax.axis_size("dp") * own_rows, local_count * 3 * hidden_width)
            .astype(jnp.bfloat16)
        )
    joined = lax.psum_scatter(partials, "dp", scatter_dimension=0, tiled=True)
    if local_count == 1:
        grad_gate, grad_up, grad_down = (
            joined[None, :, which * hidden_width : (which + 1) * hidden_width].astype(jnp.float32)
            for which in range(3)
        )
    else:
        triple_view = joined.astype(jnp.float32).reshape(-1, local_count, 3, hidden_width)
        grad_gate = jnp.transpose(triple_view[:, :, 0, :], (1, 0, 2))
        grad_up = jnp.transpose(triple_view[:, :, 1, :], (1, 0, 2))
        grad_down = jnp.transpose(triple_view[:, :, 2, :], (1, 0, 2))
    choice_rows = jnp.transpose(chosen, (1, 0, 2)).reshape(choice_count * tok_count, slot_total)
    choice_rows = choice_rows.astype(jnp.bfloat16)
    got_rows = jnp.dot(
        choice_rows, returned.reshape(slot_total, width), preferred_element_type=jnp.float32
    ).reshape(choice_count, tok_count, width)
    back_rows = jnp.dot(
        choice_rows, sent_back.reshape(slot_total, width), preferred_element_type=jnp.float32
    ).reshape(choice_count, tok_count, width)
    dy_wide = grad_out.astype(jnp.float32)
    mixed = jnp.zeros((tok_count, width), jnp.float32)
    row_sum = jnp.zeros((tok_count, width), jnp.float32)
    gate_grads = []
    for which in range(choice_count):
        got_row = got_rows[which]
        mixed = mixed + live_gate[:, which : which + 1] * got_row
        gate_grads.append(jnp.sum(dy_wide * got_row, axis=1))
        row_sum = row_sum + back_rows[which]
    layer_output = mixed.astype(jnp.bfloat16)
    gate_grad = jnp.stack(gate_grads, axis=1)
    cross_term = jnp.sum(gate_grad * gate_value, axis=1, keepdims=True)
    pick_delta = (gate_grad - cross_term) / pick_sum * picked * (1.0 - picked)
    logit_grad = jnp.sum(picker * pick_delta[:, :, None], axis=1)
    grad_tokens = (row_sum + jnp.dot(logit_grad, w_router.T, precision=highest)).astype(
        jnp.bfloat16
    )
    router_part = jnp.dot(tokens_wide.T, logit_grad, precision=highest)
    grad_router = all_sum(all_sum(router_part, "dp"), "expert")
    return (layer_output, grad_tokens, grad_router, grad_gate, grad_up, grad_down)


def solution(mesh):
    return jax.shard_map(
        on_device,
        mesh=mesh,
        in_specs=(
            P(("dp", "expert"), None),
            P(("dp", "expert"), None),
            P(("dp", "expert"), None),
            P(),
            P("expert", None, None),
            P("expert", None, None),
            P("expert", None, None),
            P(("dp", "expert"), None),
        ),
        out_specs=(
            P(("dp", "expert"), None),
            P(("dp", "expert"), None),
            P(),
            P("expert", "dp", None),
            P("expert", "dp", None),
            P("expert", "dp", None),
        ),
        check_vma=False,
    )
```
